256 devices in a mesh: fsdp: 16 (over x, y), seq: 16 (over z, core).
Axes of the slice: x: 4, y: 4, z: 8, core: 2. Of those that a mesh axis runs over, the one named last changes fastest.
Arguments:
- tokens: bfloat16 [65536, 2048], P(('fsdp', 'seq')), may hold values from -6 to 6
- seq_lengths: int32 [16, 4], P('fsdp'), may hold values from 1 to 2048, 4096 in all within a row
- in_weight: bfloat16 [2048, 6144], P(None, 'fsdp'), may hold values from -0.125 to 0.125
- short_filter: float32 [7, 6144], replicated, may hold values from -2.5 to 2.5
- long_filter: bfloat16 [128, 128], replicated, may hold values from -0.5 to 0.5
- out_weight: bfloat16 [2048, 2048], replicated, may hold values from -0.125 to 0.125
Outputs:
- mixed: bfloat16 [65536, 2048], P(('fsdp', 'seq'))
The draws below stay inside these ranges and needn't reach their ends.
Inputs may be any that keep to these rules, and one draw needn't show every extreme that they name: `seq_lengths`: in each pack the 4 lengths sum to 4096 and the longest is exactly 2048.
All inputs are finite; a program needn't handle non-finite values.
Results may differ from the reference program's by a relative error of at most 0.0073.
Values may be sent and summed in bfloat16 or wider, within the bound.
No kernel may reach another device: no remote copies, remote signals or barrier semaphores. Data moves between devices by JAX's collectives and lax.ppermute only.
A program may use at most 128 MiB of HBM per device.

```python
import math
import jax
import jax.numpy as jnp
import numpy as np
from jax import lax

D = 2048
GROUPS = 128
WIDTH = 7
FL = 128
SEQS = 4
GROUP = 4096
MOST = 2048
TOKENS = 65536
N_FSDP = 16


def block_scale(stream_key, extent, split, smallest, largest):
    gain = 1.0
    for dim, blocks in split:
        draws = jax.random.uniform(jax.random.fold_in(jax.random.fold_in(stream_key, 6), dim), (blocks,), jnp.float32, smallest / len(split), largest / len(split))
        gain = gain * jnp.repeat(jnp.exp(draws), extent[dim] // blocks).reshape((-1,) + (1,) * (len(extent) - 1 - dim))
    return gain


def split_up(number_of, total, reach, skew):
    loads = [(1 << 20) // math.isqrt(rank ** skew) + 1 for rank in range(2, number_of + 1)]
    surplus, given = total - reach - (number_of - 1), [1] * (number_of - 1)
    while surplus > 0:
        candidates = [i for i in range(number_of - 1) if given[i] < reach]
        pool, remaining = sum([loads[i] for i in candidates]), surplus
        for i in candidates:
            more = min(reach - given[i], max(1, remaining * loads[i] // pool), surplus)
            given[i] = given[i] + more
            surplus = surplus - more
    return np.array([reach] + given)


def uneven_parts(stream_key, count, total, reach, lean):
    if count == 2:
        one = jax.random.randint(stream_key, (), max(1, total - reach), min(reach, total - 1) + 1)
        return jnp.stack([one, total - one])
    lengths = jnp.asarray(split_up(count, total, reach, lean), jnp.int32)
    couples = (count - 1) // 2
    source_of, taker = lengths[1:1 + 2 * couples:2], lengths[2:2 + 2 * couples:2]
    margin = jnp.minimum(source_of - 1, reach - taker)
    passed = jax.random.randint(jax.random.fold_in(stream_key, 1), (couples,), 0, 1 << 20) % (margin + 1)
    lengths = lengths.at[1:1 + 2 * couples:2].set(source_of - passed).at[2:2 + 2 * couples:2].set(taker + passed)
    return lengths[jax.random.permutation(jax.random.fold_in(stream_key, 2), count)]


def noise(own_key, extent, deviation, most, pieces=(), kind=jnp.bfloat16):
    values = deviation * jax.random.normal(own_key, extent, jnp.float32)
    if pieces:
        values = values * block_scale(own_key, extent, pieces, -0.22, 0.18)
    return jnp.clip(values, -most, most).astype(kind)


def setup_inputs(seed: int = 0) -> dict:
    seeds = jax.random.split(jax.random.key(seed), 7)
    return {
        "tokens": noise(seeds[0], (TOKENS, D), 1.0, 6.0, ((0, 256),)),
        "seq_lengths": jax.vmap(lambda own: uneven_parts(own, SEQS, GROUP, MOST, 1))(jax.random.split(seeds[1], N_FSDP)).reshape((N_FSDP, SEQS)).astype(jnp.int32),
        "in_weight": noise(seeds[2], (D, 3 * D), D ** -0.5, 0.125, ((1, 16),)),
        "short_filter": noise(seeds[3], (WIDTH, 3 * D), 0.4, 2.5, (), jnp.float32),
        "long_filter": noise(seeds[4], (FL, GROUPS), FL ** -0.5, 0.5),
        "out_weight": noise(seeds[5], (D, D), D ** -0.5, 0.125),
    }


def filter_block(long_filter, window, position):
    filter_len, group_count = long_filter.shape
    out_rows = jnp.arange(filter_len, dtype=jnp.int32)[:, None]
    src_rows = jnp.arange(2 * filter_len - 1, dtype=jnp.int32)[None, :]
    tap_index = out_rows + (filter_len - 1) - src_rows
    inside = (tap_index >= 0) & (tap_index <= filter_len - 1) & (tap_index <= position[:, None])
    clipped = jnp.clip(tap_index, 0, filter_len - 1)
    kernel_table = jnp.where(inside[:, :, None], long_filter[clipped].astype(jnp.float32), 0.0).astype(jnp.float32)
    channels = window.shape[1]
    grouped = window.astype(jnp.float32).reshape(2 * filter_len - 1, group_count, channels // group_count)
    filtered = jnp.einsum("ijg,jgc->igc", kernel_table, grouped, precision=lax.Precision.HIGHEST)
    return filtered.reshape(filter_len, channels)


def reference(tokens, seq_lengths, in_weight, short_filter, long_filter, out_weight):
    projected = jnp.dot(tokens, in_weight, preferred_element_type=jnp.float32).astype(jnp.bfloat16)
    projected = projected.reshape(N_FSDP, GROUP, 3 * D)
    seq_starts = (jnp.cumsum(seq_lengths, axis=1) - seq_lengths).astype(jnp.int32)
    row_ids = jnp.arange(GROUP, dtype=jnp.int32)
    seq_begin = jnp.max(jnp.where(seq_starts[:, None, :] <= row_ids[None, :, None], seq_starts[:, None, :], 0), axis=2).astype(jnp.int32)
    position = row_ids[None, :] - seq_begin
    featured = jnp.zeros((N_FSDP, GROUP, 3 * D), jnp.float32)
    for tap_index in range(WIDTH):
        shifted = jnp.pad(projected, ((0, 0), (tap_index, 0), (0, 0)))[:, :GROUP].astype(jnp.float32)
        featured = featured + short_filter[tap_index] * jnp.where((position >= tap_index)[:, :, None], shifted, 0.0)
    queries = featured[:, :, :D]
    mixed_in = (featured[:, :, D:2 * D] * featured[:, :, 2 * D:]).astype(jnp.bfloat16)
    padded = jnp.pad(mixed_in, ((0, 0), (FL - 1, 0), (0, 0)))
    block_count = GROUP // FL

    def one_block(block_id):
        group_index = (block_id // block_count).astype(jnp.int32)
        first_row = ((block_id % block_count) * FL).astype(jnp.int32)
        window = lax.dynamic_slice(padded, (group_index, first_row, jnp.int32(0)), (1, 2 * FL - 1, D))[0]
        block_pos = lax.dynamic_slice(position, (group_index, first_row), (1, FL))[0]
        return filter_block(long_filter, window, block_pos)

    filtered = lax.map(one_block, jnp.arange(N_FSDP * block_count, dtype=jnp.int32))
    filtered = filtered.reshape(N_FSDP, GROUP, D)
    gated_out = (queries * filtered).astype(jnp.bfloat16).reshape(TOKENS, D)
    result = tokens.astype(jnp.float32) + jnp.dot(gated_out, out_weight, preferred_element_type=jnp.float32)
    return result.astype(jnp.bfloat16)
```

```python
import jax
import jax.numpy as jnp
from jax import lax
from jax.sharding import PartitionSpec as P

LANE = 128


def positions(row_ids, seq_starts):
    seq_begin = jnp.max(
        jnp.where(seq_starts[None, :] <= row_ids[:, None], seq_starts[None, :], 0), axis=1
    )
    return row_ids - seq_begin


def tap_table(tap_ids, long_filter):
    filter_len = long_filter.shape[0]
    one_hot = (
        tap_ids[:, :, None] == jnp.arange(filter_len, dtype=jnp.int32)[None, None, :]
    ).astype(jnp.bfloat16)
    return jnp.einsum(
        "ijt,tg->gij", one_hot, long_filter, preferred_element_type=jnp.float32
    ).astype(jnp.bfloat16)


def local(tokens, seq_lengths, in_weight, short_filter, long_filter, out_weight):
    rows, channels = tokens.shape
    width = short_filter.shape[0]
    filter_len, group_count = long_filter.shape
    per_group = channels // group_count
    n_seq = lax.axis_size("seq")
    s = lax.axis_index("seq")
    core = s % 2
    half = LANE // 2
    n_lblk = channels // LANE
    tail = filter_len + 8
    ext_rows = tail + 2 * rows

    sib_perm = [(i, i ^ 1) for i in range(n_seq)]
    sib_tokens = lax.ppermute(tokens, "seq", sib_perm)
    first = jnp.where(core == 0, tokens, sib_tokens)
    second = jnp.where(core == 0, sib_tokens, tokens)
    tail_src = tokens[rows - tail :]
    to_even = [(i - 1, i) for i in range(2, n_seq, 2)]
    to_odd = [(i - 2, i) for i in range(3, n_seq, 2)]
    tail_a = lax.ppermute(tail_src, "seq", to_even)
    tail_b = lax.ppermute(tail_src, "seq", to_odd)
    tail_tok = jnp.where(core == 0, tail_a, tail_b)
    ext_tokens = jnp.concatenate([tail_tok, first, second], axis=0)

    lengths_row = seq_lengths[0]
    seq_starts = jnp.cumsum(lengths_row) - lengths_row
    pair_start = (s // 2) * (2 * rows)
    row_ids = pair_start - tail + jnp.arange(ext_rows, dtype=jnp.int32)
    position = positions(row_ids, seq_starts)

    offset = core * half
    w_t = in_weight.T.reshape(in_weight.shape[1] // LANE, LANE, channels)
    w_part = lax.dynamic_slice_in_dim(w_t, offset, half, axis=1)
    w_all = lax.all_gather(w_part, "fsdp", axis=0, tiled=True)
    w_all = w_all.reshape(3 * n_lblk * half, channels)
    own = 3 * n_lblk * half // 3

    projected = jnp.dot(
        ext_tokens, w_all.T, preferred_element_type=jnp.float32
    ).astype(jnp.bfloat16)

    taps = short_filter.reshape(width, 3, n_lblk, LANE)
    taps = lax.dynamic_slice_in_dim(taps, offset, half, axis=3).reshape(width, 3 * own)

    start = 8
    feat_rows = ext_rows - start
    pos_f = position[start:]
    featured = jnp.zeros((feat_rows, 3 * own), jnp.float32)
    for tap_index in range(width):
        part = projected[start - tap_index : ext_rows - tap_index].astype(jnp.float32)
        featured = featured + taps[tap_index] * jnp.where(
            (pos_f >= tap_index)[:, None], part, 0.0
        )
    queries = featured[feat_rows - 2 * rows :, :own]
    mixed_in = (featured[:, own : 2 * own] * featured[:, 2 * own :]).astype(jnp.bfloat16)

    sub = LANE // per_group
    lf = long_filter.reshape(filter_len, n_lblk, sub)
    lf = lax.dynamic_slice_in_dim(lf, offset // per_group, half // per_group, axis=2)
    lf = lf.reshape(filter_len, own // per_group)
    n_groups = own // per_group

    out_rows = jnp.arange(filter_len, dtype=jnp.int32)[:, None]
    src_rows = jnp.arange(filter_len, dtype=jnp.int32)[None, :]
    cur_tap = out_rows - src_rows
    prev_tap = out_rows + filter_len - src_rows
    cur_table = tap_table(cur_tap, lf)
    prev_table = tap_table(prev_tap, lf)

    n_blocks = 2 * rows // filter_len
    mi_blocks = mixed_in.reshape(n_blocks + 1, filter_len, n_groups, per_group)
    pos_out = position[tail:].reshape(n_blocks, filter_len)
    cur_kernel = jnp.where(
        (cur_tap[None] <= pos_out[:, :, None])[:, None], cur_table[None], 0.0
    ).astype(jnp.bfloat16)
    prev_kernel = jnp.where(
        (prev_tap[None] <= pos_out[:, :, None])[:, None], prev_table[None], 0.0
    ).astype(jnp.bfloat16)
    filtered = jnp.einsum(
        "bgij,bjgc->bigc", cur_kernel, mi_blocks[1:], preferred_element_type=jnp.float32
    )
    filtered = filtered + jnp.einsum(
        "bgij,bjgc->bigc", prev_kernel, mi_blocks[:-1], preferred_element_type=jnp.float32
    )
    filtered = filtered.reshape(2 * rows, own)
    gated = (queries * filtered).astype(jnp.bfloat16)

    mine = jnp.where(core == 0, gated[:rows], gated[rows:])
    theirs = jnp.where(core == 0, gated[rows:], gated[:rows])
    from_sib = lax.ppermute(theirs, "seq", sib_perm)
    ow = out_weight.reshape(n_lblk, LANE, channels)
    ow_own = lax.dynamic_slice_in_dim(ow, offset, half, axis=1).reshape(own, channels)
    ow_sib = lax.dynamic_slice_in_dim(ow, half - offset, half, axis=1).reshape(own, channels)
    result = tokens.astype(jnp.float32) + jnp.dot(
        jnp.concatenate([mine, from_sib], axis=1),
        jnp.concatenate([ow_own, ow_sib], axis=0),
        preferred_element_type=jnp.float32,
    )
    return result.astype(jnp.bfloat16)


def solution(mesh):
    in_specs = (P(("fsdp", "seq"), None), P("fsdp", None), P(None, "fsdp"), P(), P(), P())
    out_specs = P(("fsdp", "seq"), None)
    return jax.shard_map(local, mesh=mesh, in_specs=in_specs, out_specs=out_specs, check_vma=False)
```

```python
import jax
import jax.numpy as jnp
from jax import lax
from jax.sharding import PartitionSpec as P

LANE = 128
N_CHUNK = 2


def positions(row_ids, seq_starts):
    seq_begin = jnp.max(
        jnp.where(seq_starts[None, :] <= row_ids[:, None], seq_starts[None, :], 0), axis=1
    )
    return row_ids - seq_begin


def tap_table(tap_ids, long_filter):
    filter_len = long_filter.shape[0]
    one_hot = (
        tap_ids[:, :, None] == jnp.arange(filter_len, dtype=jnp.int32)[None, None, :]
    ).astype(jnp.bfloat16)
    return jnp.einsum(
        "ijt,tg->gij", one_hot, long_filter, preferred_element_type=jnp.float32
    ).astype(jnp.bfloat16)


def local(tokens, seq_lengths, in_weight, short_filter, long_filter, out_weight):
    rows, channels = tokens.shape
    width = short_filter.shape[0]
    filter_len, group_count = long_filter.shape
    per_group = channels // group_count
    n_seq = lax.axis_size("seq")
    s = lax.axis_index("seq")
    core = s % 2
    half = LANE // 2
    n_lblk = channels // LANE
    tail = filter_len + 8
    ext_rows = tail + 2 * rows

    sib_perm = [(i, i ^ 1) for i in range(n_seq)]
    sib_tokens = lax.ppermute(tokens, "seq", sib_perm)
    first = jnp.where(core == 0, tokens, sib_tokens)
    second = jnp.where(core == 0, sib_tokens, tokens)
    tail_src = tokens[rows - tail :]
    to_even = [(i - 1, i) for i in range(2, n_seq, 2)]
    to_odd = [(i - 2, i) for i in range(3, n_seq, 2)]
    tail_a = lax.ppermute(tail_src, "seq", to_even)
    tail_b = lax.ppermute(tail_src, "seq", to_odd)
    tail_tok = jnp.where(core == 0, tail_a, tail_b)
    ext_tokens = jnp.concatenate([tail_tok, first, second], axis=0)

    lengths_row = seq_lengths[0]
    seq_starts = jnp.cumsum(lengths_row) - lengths_row
    pair_start = (s // 2) * (2 * rows)
    row_ids = pair_start - tail + jnp.arange(ext_rows, dtype=jnp.int32)
    position = positions(row_ids, seq_starts)

    n_chunk = N_CHUNK
    w = half // n_chunk
    own = 3 * n_lblk * w // 3
    n_groups = own // per_group
    sub = LANE // per_group
    w_t = in_weight.T.reshape(in_weight.shape[1] // LANE, LANE, channels)
    taps_all = short_filter.reshape(width, 3, n_lblk, LANE)
    lf_all = long_filter.reshape(filter_len, n_lblk, sub)
    ow = out_weight.reshape(n_lblk, LANE, channels)

    start = 8
    feat_rows = ext_rows - start
    pos_f = position[start:]
    out_rows = jnp.arange(filter_len, dtype=jnp.int32)[:, None]
    src_rows = jnp.arange(filter_len, dtype=jnp.int32)[None, :]
    cur_tap = out_rows - src_rows
    prev_tap = out_rows + filter_len - src_rows
    n_blocks = 2 * rows // filter_len
    pos_out = position[tail:].reshape(n_blocks, filter_len)
    cur_mask = (cur_tap[None] <= pos_out[:, :, None])[:, None]
    prev_mask = (prev_tap[None] <= pos_out[:, :, None])[:, None]

    pieces = []
    for chunk in range(n_chunk):
        offset = core * half + chunk * w
        w_part = lax.dynamic_slice_in_dim(w_t, offset, w, axis=1)
        w_all = lax.all_gather(w_part, "fsdp", axis=0, tiled=True)
        w_all = w_all.reshape(3 * own, channels)
        projected = jnp.dot(
            ext_tokens, w_all.T, preferred_element_type=jnp.float32
        ).astype(jnp.bfloat16)
        taps = lax.dynamic_slice_in_dim(taps_all, offset, w, axis=3).reshape(width, 3 * own)
        featured = jnp.zeros((feat_rows, 3 * own), jnp.float32)
        for tap_index in range(width):
            part = projected[start - tap_index : ext_rows - tap_index].astype(jnp.float32)
            featured = featured + taps[tap_index] * jnp.where(
                (pos_f >= tap_index)[:, None], part, 0.0
            )
        queries = featured[feat_rows - 2 * rows :, :own]
        mixed_in = (featured[:, own : 2 * own] * featured[:, 2 * own :]).astype(jnp.bfloat16)

        lf = lax.dynamic_slice_in_dim(lf_all, offset // per_group, w // per_group, axis=2)
        lf = lf.reshape(filter_len, n_groups)
        cur_table = tap_table(cur_tap, lf)
        prev_table = tap_table(prev_tap, lf)
        mi_blocks = mixed_in.reshape(n_blocks + 1, filter_len, n_groups, per_group)
        cur_kernel = jnp.where(cur_mask, cur_table[None], 0.0).astype(jnp.bfloat16)
        prev_kernel = jnp.where(prev_mask, prev_table[None], 0.0).astype(jnp.bfloat16)
        filtered = jnp.einsum(
            "bgij,bjgc->bigc", cur_kernel, mi_blocks[1:], preferred_element_type=jnp.float32
        )
        filtered = filtered + jnp.einsum(
            "bgij,bjgc->bigc", prev_kernel, mi_blocks[:-1], preferred_element_type=jnp.float32
        )
        filtered = filtered.reshape(2 * rows, own)
        gated = (queries * filtered).astype(jnp.bfloat16)

        mine = jnp.where(core == 0, gated[:rows], gated[rows:])
        theirs = jnp.where(core == 0, gated[rows:], gated[:rows])
        from_sib = lax.ppermute(theirs, "seq", sib_perm)
        sib_offset = (1 - core) * half + chunk * w
        ow_own = lax.dynamic_slice_in_dim(ow, offset, w, axis=1).reshape(own, channels)
        ow_sib = lax.dynamic_slice_in_dim(ow, sib_offset, w, axis=1).reshape(own, channels)
        pieces.append(jnp.dot(
            jnp.concatenate([mine, from_sib], axis=1),
            jnp.concatenate([ow_own, ow_sib], axis=0),
            preferred_element_type=jnp.float32,
        ))
    mixed = pieces[0]
    for piece in pieces[1:]:
        mixed = mixed + piece
    result = tokens.astype(jnp.float32) + mixed
    return result.astype(jnp.bfloat16)


def solution(mesh):
    in_specs = (P(("fsdp", "seq"), None), P("fsdp", None), P(None, "fsdp"), P(), P(), P())
    out_specs = P(("fsdp", "seq"), None)
    return jax.shard_map(local, mesh=mesh, in_specs=in_specs, out_specs=out_specs, check_vma=False)
```

```python
import jax
import jax.numpy as jnp
from jax import lax
from jax.sharding import PartitionSpec as P

LANE = 128
GROUP_DEVS = 4


def positions(row_ids, seq_starts):
    seq_begin = jnp.max(
        jnp.where(seq_starts[None, :] <= row_ids[:, None], seq_starts[None, :], 0), axis=1
    )
    return row_ids - seq_begin


def tap_table(tap_ids, long_filter):
    filter_len = long_filter.shape[0]
    one_hot = (
        tap_ids[:, :, None] == jnp.arange(filter_len, dtype=jnp.int32)[None, None, :]
    ).astype(jnp.bfloat16)
    return jnp.einsum(
        "ijt,tg->gij", one_hot, long_filter, preferred_element_type=jnp.float32
    ).astype(jnp.bfloat16)


def local(tokens, seq_lengths, in_weight, short_filter, long_filter, out_weight):
    rows, channels = tokens.shape
    width = short_filter.shape[0]
    filter_len, group_count = long_filter.shape
    per_group = channels // group_count
    n_seq = lax.axis_size("seq")
    s = lax.axis_index("seq")
    member = s % GROUP_DEVS
    part = LANE // GROUP_DEVS
    n_lblk = channels // LANE
    tail = filter_len + 8
    span = GROUP_DEVS * rows
    ext_rows = tail + span

    swaps = [[(i, i ^ d) for i in range(n_seq)] for d in range(1, GROUP_DEVS)]
    from_member = [tokens] + [lax.ppermute(tokens, "seq", perm) for perm in swaps]
    blocks = []
    for m in range(GROUP_DEVS):
        pick = from_member[0]
        for d in range(1, GROUP_DEVS):
            pick = jnp.where((member ^ d) == m, from_member[d], pick)
        blocks.append(pick)
    tail_src = tokens[rows - tail :]
    tail_tok = jnp.zeros_like(tail_src)
    for m in range(GROUP_DEVS):
        dist = m + 1
        perm = [(i - dist, i) for i in range(GROUP_DEVS, n_seq) if i % GROUP_DEVS == m]
        got = lax.ppermute(tail_src, "seq", perm)
        tail_tok = jnp.where(member == m, got, tail_tok)
    ext_tokens = jnp.concatenate([tail_tok] + blocks, axis=0)

    lengths_row = seq_lengths[0]
    seq_starts = jnp.cumsum(lengths_row) - lengths_row
    pair_start = (s // GROUP_DEVS) * span
    row_ids = pair_start - tail + jnp.arange(ext_rows, dtype=jnp.int32)
    position = positions(row_ids, seq_starts)

    offset = member * part
    w_t = in_weight.T.reshape(in_weight.shape[1] // LANE, LANE, channels)
    w_part = lax.dynamic_slice_in_dim(w_t, offset, part, axis=1)
    w_all = lax.all_gather(w_part, "fsdp", axis=0, tiled=True)
    own = n_lblk * part
    w_all = w_all.reshape(3 * own, channels)

    projected = jnp.dot(
        ext_tokens, w_all.T, preferred_element_type=jnp.float32
    ).astype(jnp.bfloat16)

    taps = short_filter.reshape(width, 3, n_lblk, LANE)
    taps = lax.dynamic_slice_in_dim(taps, offset, part, axis=3).reshape(width, 3 * own)

    start = 8
    feat_rows = ext_rows - start
    pos_f = position[start:]
    featured = jnp.zeros((feat_rows, 3 * own), jnp.float32)
    for tap_index in range(width):
        shifted = projected[start - tap_index : ext_rows - tap_index].astype(jnp.float32)
        featured = featured + taps[tap_index] * jnp.where(
            (pos_f >= tap_index)[:, None], shifted, 0.0
        )
    queries = featured[feat_rows - span :, :own]
    mixed_in = (featured[:, own : 2 * own] * featured[:, 2 * own :]).astype(jnp.bfloat16)

    sub = LANE // per_group
    lf = long_filter.reshape(filter_len, n_lblk, sub)
    lf = lax.dynamic_slice_in_dim(lf, offset // per_group, part // per_group, axis=2)
    lf = lf.reshape(filter_len, own // per_group)
    n_groups = own // per_group

    out_rows = jnp.arange(filter_len, dtype=jnp.int32)[:, None]
    src_rows = jnp.arange(filter_len, dtype=jnp.int32)[None, :]
    cur_tap = out_rows - src_rows
    prev_tap = out_rows + filter_len - src_rows
    cur_table = tap_table(cur_tap, lf)
    prev_table = tap_table(prev_tap, lf)

    n_blocks = span // filter_len
    mi_blocks = mixed_in.reshape(n_blocks + 1, filter_len, n_groups, per_group)
    pos_out = position[tail:].reshape(n_blocks, filter_len)
    cur_kernel = jnp.where(
        (cur_tap[None] <= pos_out[:, :, None])[:, None], cur_table[None], 0.0
    ).astype(jnp.bfloat16)
    prev_kernel = jnp.where(
        (prev_tap[None] <= pos_out[:, :, None])[:, None], prev_table[None], 0.0
    ).astype(jnp.bfloat16)
    filtered = jnp.einsum(
        "bgij,bjgc->bigc", cur_kernel, mi_blocks[1:], preferred_element_type=jnp.float32
    )
    filtered = filtered + jnp.einsum(
        "bgij,bjgc->bigc", prev_kernel, mi_blocks[:-1], preferred_element_type=jnp.float32
    )
    filtered = filtered.reshape(span, own)
    gated = (queries * filtered).astype(jnp.bfloat16)

    gated = gated.reshape(GROUP_DEVS, rows, own)
    ow = out_weight.reshape(n_lblk, LANE, channels)
    pieces = []
    weights = []
    for d in range(GROUP_DEVS):
        send = lax.dynamic_index_in_dim(gated, member ^ d, axis=0, keepdims=False)
        got = send if d == 0 else lax.ppermute(send, "seq", swaps[d - 1])
        pieces.append(got)
        src_offset = (member ^ d) * part
        weights.append(lax.dynamic_slice_in_dim(ow, src_offset, part, axis=1).reshape(own, channels))
    result = tokens.astype(jnp.float32) + jnp.dot(
        jnp.concatenate(pieces, axis=1),
        jnp.concatenate(weights, axis=0),
        preferred_element_type=jnp.float32,
    )
    return result.astype(jnp.bfloat16)


def solution(mesh):
    in_specs = (P(("fsdp", "seq"), None), P("fsdp", None), P(None, "fsdp"), P(), P(), P())
    out_specs = P(("fsdp", "seq"), None)
    return jax.shard_map(local, mesh=mesh, in_specs=in_specs, out_specs=out_specs, check_vma=False)
```

```python
import jax
import jax.numpy as jnp
from jax import lax
from jax.sharding import PartitionSpec as P

LANE = 128
GROUP_DEVS = 4


def positions(row_ids, seq_starts):
    seq_begin = jnp.max(
        jnp.where(seq_starts[None, :] <= row_ids[:, None], seq_starts[None, :], 0), axis=1
    )
    return row_ids - seq_begin


def tap_table(tap_ids, long_filter):
    filter_len = long_filter.shape[0]
    one_hot = (
        tap_ids[:, :, None] == jnp.arange(filter_len, dtype=jnp.int32)[None, None, :]
    ).astype(jnp.bfloat16)
    return jnp.einsum(
        "ijt,tg->gij", one_hot, long_filter, preferred_element_type=jnp.float32
    ).astype(jnp.bfloat16)


def local(tokens, seq_lengths, in_weight, short_filter, long_filter, out_weight):
    rows, channels = tokens.shape
    width = short_filter.shape[0]
    filter_len, group_count = long_filter.shape
    per_group = channels // group_count
    n_seq = lax.axis_size("seq")
    s = lax.axis_index("seq")
    member = s % GROUP_DEVS
    part = LANE // GROUP_DEVS
    n_lblk = channels // LANE
    tail = filter_len + 8
    span = GROUP_DEVS * rows
    ext_rows = tail + span

    swaps = [[(i, i ^ d) for i in range(n_seq)] for d in range(1, GROUP_DEVS)]
    from_member = [tokens] + [lax.ppermute(tokens, "seq", perm) for perm in swaps]
    blocks = []
    for m in range(GROUP_DEVS):
        pick = from_member[0]
        for d in range(1, GROUP_DEVS):
            pick = jnp.where((member ^ d) == m, from_member[d], pick)
        blocks.append(pick)
    tail_src = tokens[rows - tail :]
    tail_tok = jnp.zeros_like(tail_src)
    for m in range(GROUP_DEVS):
        dist = m + 1
        perm = [(i - dist, i) for i in range(GROUP_DEVS, n_seq) if i % GROUP_DEVS == m]
        got = lax.ppermute(tail_src, "seq", perm)
        tail_tok = jnp.where(member == m, got, tail_tok)
    ext_tokens = jnp.concatenate([tail_tok] + blocks, axis=0)

    lengths_row = seq_lengths[0]
    seq_starts = jnp.cumsum(lengths_row) - lengths_row
    pair_start = (s // GROUP_DEVS) * span
    row_ids = pair_start - tail + jnp.arange(ext_rows, dtype=jnp.int32)
    position = positions(row_ids, seq_starts)

    offset = member * part
    w_t = in_weight.T.reshape(in_weight.shape[1] // LANE, LANE, channels)
    w_part = lax.dynamic_slice_in_dim(w_t, offset, part, axis=1)
    w_all = lax.all_gather(w_part, "fsdp", axis=0, tiled=True)
    own = n_lblk * part
    w_all = w_all.reshape(3 * own, channels)

    ow = out_weight.reshape(n_lblk, LANE, channels)
    weights = []
    for d in range(GROUP_DEVS):
        src_offset = (member ^ d) * part
        weights.append(lax.dynamic_slice_in_dim(ow, src_offset, part, axis=1).reshape(own, channels))
    ow_cat = jnp.concatenate(weights, axis=0)
    ext_tokens, ow_cat = lax.optimization_barrier((ext_tokens, ow_cat))
    projected = jnp.dot(
        ext_tokens, w_all.T, preferred_element_type=jnp.float32
    ).astype(jnp.bfloat16)

    taps = short_filter.reshape(width, 3, n_lblk, LANE)
    taps = lax.dynamic_slice_in_dim(taps, offset, part, axis=3).reshape(width, 3 * own)

    start = 8
    feat_rows = ext_rows - start
    pos_f = position[start:]
    featured = jnp.zeros((feat_rows, 3 * own), jnp.float32)
    for tap_index in range(width):
        shifted = projected[start - tap_index : ext_rows - tap_index].astype(jnp.float32)
        featured = featured + taps[tap_index] * jnp.where(
            (pos_f >= tap_index)[:, None], shifted, 0.0
        )
    queries = featured[feat_rows - span :, :own]
    mixed_in = (featured[:, own : 2 * own] * featured[:, 2 * own :]).astype(jnp.bfloat16)

    sub = LANE // per_group
    lf = long_filter.reshape(filter_len, n_lblk, sub)
    lf = lax.dynamic_slice_in_dim(lf, offset // per_group, part // per_group, axis=2)
    lf = lf.reshape(filter_len, own // per_group)
    n_groups = own // per_group

    out_rows = jnp.arange(filter_len, dtype=jnp.int32)[:, None]
    src_rows = jnp.arange(filter_len, dtype=jnp.int32)[None, :]
    cur_tap = out_rows - src_rows
    prev_tap = out_rows + filter_len - src_rows
    cur_table = tap_table(cur_tap, lf)
    prev_table = tap_table(prev_tap, lf)

    n_blocks = span // filter_len
    pos_out = position[tail:].reshape(n_blocks, filter_len)
    cur_kernel = jnp.where(
        (cur_tap[None] <= pos_out[:, :, None])[:, None], cur_table[None], 0.0
    ).astype(jnp.bfloat16)
    prev_kernel = jnp.where(
        (prev_tap[None] <= pos_out[:, :, None])[:, None], prev_table[None], 0.0
    ).astype(jnp.bfloat16)

    mi_t = mixed_in.T.reshape(n_groups, per_group, n_blocks + 1, filter_len)
    filtered = jnp.einsum(
        "gcbj,bgij->gcbi", mi_t[:, :, 1:], cur_kernel, preferred_element_type=jnp.float32
    )
    filtered = filtered + jnp.einsum(
        "gcbj,bgij->gcbi", mi_t[:, :, :-1], prev_kernel, preferred_element_type=jnp.float32
    )
    filtered = filtered.reshape(own, span)
    gated = (queries.T * filtered).astype(jnp.bfloat16)


    gated = gated.reshape(own, GROUP_DEVS, rows)
    pieces = []
    for d in range(GROUP_DEVS):
        send = lax.dynamic_index_in_dim(gated, member ^ d, axis=1, keepdims=False)
        got = send if d == 0 else lax.ppermute(send, "seq", swaps[d - 1])
        pieces.append(got)
    result = tokens.astype(jnp.float32) + lax.dot_general(
        jnp.concatenate(pieces, axis=0),
        ow_cat,
        (((0,), (0,)), ((), ())),
        preferred_element_type=jnp.float32,
    )
    return result.astype(jnp.bfloat16)


def solution(mesh):
    in_specs = (P(("fsdp", "seq"), None), P("fsdp", None), P(None, "fsdp"), P(), P(), P())
    out_specs = P(("fsdp", "seq"), None)
    return jax.shard_map(local, mesh=mesh, in_specs=in_specs, out_specs=out_specs, check_vma=False)
```

```python
import jax
import jax.numpy as jnp
from jax import lax
from jax.sharding import PartitionSpec as P

LANE = 128
GROUP_DEVS = 4


def positions(row_ids, seq_starts):
    seq_begin = jnp.max(
        jnp.where(seq_starts[None, :] <= row_ids[:, None], seq_starts[None, :], 0), axis=1
    )
    return row_ids - seq_begin


def tap_table(tap_ids, long_filter):
    filter_len = long_filter.shape[0]
    one_hot = (
        tap_ids[:, :, None] == jnp.arange(filter_len, dtype=jnp.int32)[None, None, :]
    ).astype(jnp.bfloat16)
    return jnp.einsum(
        "ijt,tg->gij", one_hot, long_filter, preferred_element_type=jnp.float32
    ).astype(jnp.bfloat16)


def local(tokens, seq_lengths, in_weight, short_filter, long_filter, out_weight):
    rows, channels = tokens.shape
    width = short_filter.shape[0]
    filter_len, group_count = long_filter.shape
    per_group = channels // group_count
    n_seq = lax.axis_size("seq")
    s = lax.axis_index("seq")
    member = s % GROUP_DEVS
    part = LANE // GROUP_DEVS
    n_lblk = channels // LANE
    tail = filter_len + 8
    span = GROUP_DEVS * rows
    ext_rows = tail + span

    swaps = [[(i, i ^ d) for i in range(n_seq)] for d in range(1, GROUP_DEVS)]
    from_member = [tokens] + [lax.ppermute(tokens, "seq", perm) for perm in swaps]
    blocks = []
    for m in range(GROUP_DEVS):
        pick = from_member[0]
        for d in range(1, GROUP_DEVS):
            pick = jnp.where((member ^ d) == m, from_member[d], pick)
        blocks.append(pick)
    tail_src = tokens[rows - tail :]
    tail_tok = jnp.zeros_like(tail_src)
    for m in range(GROUP_DEVS):
        dist = m + 1
        perm = [(i - dist, i) for i in range(GROUP_DEVS, n_seq) if i % GROUP_DEVS == m]
        got = lax.ppermute(tail_src, "seq", perm)
        tail_tok = jnp.where(member == m, got, tail_tok)
    ext_tokens = jnp.concatenate([tail_tok] + blocks, axis=0)

    lengths_row = seq_lengths[0]
    seq_starts = jnp.cumsum(lengths_row) - lengths_row
    pair_start = (s // GROUP_DEVS) * span
    row_ids = pair_start - tail + jnp.arange(ext_rows, dtype=jnp.int32)
    position = positions(row_ids, seq_starts)

    offset = member * part
    w_t = in_weight.T.reshape(in_weight.shape[1] // LANE, LANE, channels)
    w_part = lax.dynamic_slice_in_dim(w_t, offset, part, axis=1)
    w_all = lax.all_gather(w_part, "fsdp", axis=0, tiled=True)
    own = n_lblk * part
    w_all = w_all.reshape(3 * own, channels)

    ow = out_weight.reshape(n_lblk, LANE, channels)
    weights = []
    for d in range(GROUP_DEVS):
        src_offset = (member ^ d) * part
        weights.append(lax.dynamic_slice_in_dim(ow, src_offset, part, axis=1).reshape(own, channels))
    ow_cat = jnp.concatenate(weights, axis=0)
    ext_tokens, ow_cat = lax.optimization_barrier((ext_tokens, ow_cat))
    projected = jnp.dot(
        ext_tokens, w_all.T, preferred_element_type=jnp.float32
    ).astype(jnp.bfloat16)

    taps = short_filter.reshape(width, 3, n_lblk, LANE)
    taps = lax.dynamic_slice_in_dim(taps, offset, part, axis=3).reshape(width, 3 * own)

    start = 8
    pos_f = position[start:]
    pos_q = position[tail:]

    def featurize(first, lo, hi, pos):
        total = None
        for tap_index in range(width):
            shifted = projected[first - tap_index : ext_rows - tap_index, lo:hi].astype(jnp.float32)
            term = taps[tap_index, lo:hi] * jnp.where((pos >= tap_index)[:, None], shifted, 0.0)
            total = term if total is None else total + term
        return total

    queries = featurize(tail, 0, own, pos_q)
    mixed_in = (
        featurize(start, own, 2 * own, pos_f) * featurize(start, 2 * own, 3 * own, pos_f)
    ).astype(jnp.bfloat16)

    sub = LANE // per_group
    lf = long_filter.reshape(filter_len, n_lblk, sub)
    lf = lax.dynamic_slice_in_dim(lf, offset // per_group, part // per_group, axis=2)
    lf = lf.reshape(filter_len, own // per_group)
    n_groups = own // per_group

    out_rows = jnp.arange(filter_len, dtype=jnp.int32)[:, None]
    src_rows = jnp.arange(filter_len, dtype=jnp.int32)[None, :]
    cur_tap = out_rows - src_rows
    prev_tap = out_rows + filter_len - src_rows
    cur_table = tap_table(cur_tap, lf)
    prev_table = tap_table(prev_tap, lf)

    n_blocks = span // filter_len
    pos_out = position[tail:].reshape(n_blocks, filter_len)
    cur_kernel = jnp.where(
        (cur_tap[None] <= pos_out[:, :, None])[:, None], cur_table[None], 0.0
    ).astype(jnp.bfloat16)
    prev_kernel = jnp.where(
        (prev_tap[None] <= pos_out[:, :, None])[:, None], prev_table[None], 0.0
    ).astype(jnp.bfloat16)

    mi_t = mixed_in.T.reshape(n_groups, per_group, n_blocks + 1, filter_len)
    filtered = jnp.einsum(
        "gcbj,bgij->gbci", mi_t[:, :, 1:], cur_kernel, preferred_element_type=jnp.float32
    )
    filtered = filtered + jnp.einsum(
        "gcbj,bgij->gbci", mi_t[:, :, :-1], prev_kernel, preferred_element_type=jnp.float32
    )
    q_t = queries.reshape(n_blocks, filter_len, n_groups, per_group).transpose(2, 0, 3, 1)
    gated = (q_t * filtered).astype(jnp.bfloat16)

    per_member = rows // filter_len
    gated = gated.reshape(n_groups, GROUP_DEVS, per_member, per_group, filter_len)
    ow_cat = ow_cat.reshape(GROUP_DEVS, n_groups, per_group, channels)
    result = tokens.astype(jnp.float32)
    for d in range(GROUP_DEVS):
        send = lax.dynamic_index_in_dim(gated, member ^ d, axis=1, keepdims=False)
        got = send if d == 0 else lax.ppermute(send, "seq", swaps[d - 1])
        part_out = lax.dot_general(
            got, ow_cat[d], (((0, 2), (0, 1)), ((), ())), preferred_element_type=jnp.float32
        )
        result = result + part_out.reshape(rows, channels)
    return result.astype(jnp.bfloat16)


def solution(mesh):
    in_specs = (P(("fsdp", "seq"), None), P("fsdp", None), P(None, "fsdp"), P(), P(), P())
    out_specs = P(("fsdp", "seq"), None)
    return jax.shard_map(local, mesh=mesh, in_specs=in_specs, out_specs=out_specs, check_vma=False)
```

```python
import jax
import jax.numpy as jnp
from jax import lax
from jax.sharding import PartitionSpec as P

LANE = 128
GROUP_DEVS = 4
SEQ = ("z", "c")
SEQ_SIZE = 16


def positions(row_ids, seq_starts):
    seq_begin = jnp.max(
        jnp.where(seq_starts[None, :] <= row_ids[:, None], seq_starts[None, :], 0), axis=1
    )
    return row_ids - seq_begin


def tap_table(tap_ids, long_filter):
    filter_len = long_filter.shape[0]
    one_hot = (
        tap_ids[:, :, None] == jnp.arange(filter_len, dtype=jnp.int32)[None, None, :]
    ).astype(jnp.bfloat16)
    return jnp.einsum(
        "ijt,tg->gij", one_hot, long_filter, preferred_element_type=jnp.float32
    ).astype(jnp.bfloat16)


def ring_gather(piece, axis, split_axis, into_axis):
    n = 4
    pos = lax.axis_index(axis)
    fwd = [(i, (i + 1) % n) for i in range(n)]
    bwd = [(i, (i - 1) % n) for i in range(n)]
    from_prev = lax.ppermute(piece, axis, fwd)
    from_next = lax.ppermute(piece, axis, bwd)
    h = piece.shape[split_axis] // 2
    far_a = lax.ppermute(lax.slice_in_dim(from_prev, 0, h, axis=split_axis), axis, fwd)
    far_b = lax.ppermute(lax.slice_in_dim(from_next, h, 2 * h, axis=split_axis), axis, bwd)
    far = jnp.concatenate([far_a, far_b], axis=split_axis)
    shape = piece.shape[:into_axis] + (n,) + piece.shape[into_axis:]
    out = jnp.zeros(shape, piece.dtype)
    for step, block in ((0, piece), (n - 1, from_prev), (1, from_next), (2, far)):
        out = lax.dynamic_update_index_in_dim(out, block, (pos + step) % n, axis=into_axis)
    return out


def local(tokens, seq_lengths, in_weight, short_filter, long_filter, out_weight):
    rows, channels = tokens.shape
    width = short_filter.shape[0]
    filter_len, group_count = long_filter.shape
    per_group = channels // group_count
    n_seq = SEQ_SIZE
    s = lax.axis_index(SEQ)
    member = s % GROUP_DEVS
    part = LANE // GROUP_DEVS
    n_lblk = channels // LANE
    tail = filter_len + 8
    span = GROUP_DEVS * rows
    ext_rows = tail + span

    swaps = [[(i, i ^ d) for i in range(n_seq)] for d in range(1, GROUP_DEVS)]
    from_member = [tokens] + [lax.ppermute(tokens, SEQ, perm) for perm in swaps]
    blocks = []
    for m in range(GROUP_DEVS):
        pick = from_member[0]
        for d in range(1, GROUP_DEVS):
            pick = jnp.where((member ^ d) == m, from_member[d], pick)
        blocks.append(pick)
    tail_src = tokens[rows - tail :]
    tail_tok = jnp.zeros_like(tail_src)
    for m in range(GROUP_DEVS):
        dist = m + 1
        perm = [(i - dist, i) for i in range(GROUP_DEVS, n_seq) if i % GROUP_DEVS == m]
        got = lax.ppermute(tail_src, SEQ, perm)
        tail_tok = jnp.where(member == m, got, tail_tok)
    ext_tokens = jnp.concatenate([tail_tok] + blocks, axis=0)

    lengths_row = seq_lengths[0]
    seq_starts = jnp.cumsum(lengths_row) - lengths_row
    pair_start = (s // GROUP_DEVS) * span
    row_ids = pair_start - tail + jnp.arange(ext_rows, dtype=jnp.int32)
    position = positions(row_ids, seq_starts)

    offset = member * part
    w_t = in_weight.T.reshape(in_weight.shape[1] // LANE, LANE, channels)
    w_part = lax.dynamic_slice_in_dim(w_t, offset, part, axis=1)
    own = n_lblk * part
    lo = channels // 2
    a1 = ring_gather(w_part[:, :, :lo], "x", 1, 0)
    b1 = ring_gather(w_part[:, :, lo:], "y", 1, 0)
    w_lo = ring_gather(a1, "y", 0, 1).reshape(3 * own, lo)
    w_hi = ring_gather(b1, "x", 0, 0).reshape(3 * own, channels - lo)

    ow = out_weight.reshape(n_lblk, LANE, channels)
    weights = []
    for d in range(GROUP_DEVS):
        src_offset = (member ^ d) * part
        weights.append(lax.dynamic_slice_in_dim(ow, src_offset, part, axis=1).reshape(own, channels))
    ow_cat = jnp.concatenate(weights, axis=0)
    ext_tokens, ow_cat = lax.optimization_barrier((ext_tokens, ow_cat))
    projected = (
        jnp.dot(ext_tokens[:, :lo], w_lo.T, preferred_element_type=jnp.float32)
        + jnp.dot(ext_tokens[:, lo:], w_hi.T, preferred_element_type=jnp.float32)
    ).astype(jnp.bfloat16)

    taps = short_filter.reshape(width, 3, n_lblk, LANE)
    taps = lax.dynamic_slice_in_dim(taps, offset, part, axis=3).reshape(width, 3 * own)

    start = 8
    feat_rows = ext_rows - start
    pos_f = position[start:]
    featured = jnp.zeros((feat_rows, 3 * own), jnp.float32)
    for tap_index in range(width):
        shifted = projected[start - tap_index : ext_rows - tap_index].astype(jnp.float32)
        featured = featured + taps[tap_index] * jnp.where(
            (pos_f >= tap_index)[:, None], shifted, 0.0
        )
    queries = featured[feat_rows - span :, :own]
    mixed_in = (featured[:, own : 2 * own] * featured[:, 2 * own :]).astype(jnp.bfloat16)

    sub = LANE // per_group
    lf = long_filter.reshape(filter_len, n_lblk, sub)
    lf = lax.dynamic_slice_in_dim(lf, offset // per_group, part // per_group, axis=2)
    lf = lf.reshape(filter_len, own // per_group)
    n_groups = own // per_group

    out_rows = jnp.arange(filter_len, dtype=jnp.int32)[:, None]
    src_rows = jnp.arange(filter_len, dtype=jnp.int32)[None, :]
    cur_tap = out_rows - src_rows
    prev_tap = out_rows + filter_len - src_rows
    cur_table = tap_table(cur_tap, lf)
    prev_table = tap_table(prev_tap, lf)

    n_blocks = span // filter_len
    pos_out = position[tail:].reshape(n_blocks, filter_len)
    cur_kernel = jnp.where(
        (cur_tap[None] <= pos_out[:, :, None])[:, None], cur_table[None], 0.0
    ).astype(jnp.bfloat16)
    prev_kernel = jnp.where(
        (prev_tap[None] <= pos_out[:, :, None])[:, None], prev_table[None], 0.0
    ).astype(jnp.bfloat16)

    mi_t = mixed_in.T.reshape(n_groups, per_group, n_blocks + 1, filter_len)
    filtered = jnp.einsum(
        "gcbj,bgij->gcbi", mi_t[:, :, 1:], cur_kernel, preferred_element_type=jnp.float32
    )
    filtered = filtered + jnp.einsum(
        "gcbj,bgij->gcbi", mi_t[:, :, :-1], prev_kernel, preferred_element_type=jnp.float32
    )
    filtered = filtered.reshape(own, span)
    gated = (queries.T * filtered).astype(jnp.bfloat16)


    gated = gated.reshape(own, GROUP_DEVS, rows)
    pieces = []
    for d in range(GROUP_DEVS):
        send = lax.dynamic_index_in_dim(gated, member ^ d, axis=1, keepdims=False)
        got = send if d == 0 else lax.ppermute(send, SEQ, swaps[d - 1])
        pieces.append(got)
    result = tokens.astype(jnp.float32) + lax.dot_general(
        jnp.concatenate(pieces, axis=0),
        ow_cat,
        (((0,), (0,)), ((), ())),
        preferred_element_type=jnp.float32,
    )
    return result.astype(jnp.bfloat16)


def solution(mesh):
    fsdp, seq = mesh.devices.shape
    devices = mesh.devices.reshape(4, fsdp // 4, seq // 2, 2)
    mesh4 = jax.sharding.Mesh(devices, ("x", "y", "z", "c"))
    rows_spec = P(("x", "y", "z", "c"), None)
    in_specs = (rows_spec, P(("x", "y"), None), P(None, ("x", "y")), P(), P(), P())
    return jax.shard_map(local, mesh=mesh4, in_specs=in_specs, out_specs=rows_spec, check_vma=False)
```

```python
import jax
import jax.numpy as jnp
from jax import lax
from jax.sharding import PartitionSpec as P

LANE = 128
GROUP_DEVS = 4


def positions(row_ids, seq_starts):
    seq_begin = jnp.max(
        jnp.where(seq_starts[None, :] <= row_ids[:, None], seq_starts[None, :], 0), axis=1
    )
    return row_ids - seq_begin


def tap_table(tap_ids, long_filter):
    filter_len = long_filter.shape[0]
    one_hot = (
        tap_ids[:, :, None] == jnp.arange(filter_len, dtype=jnp.int32)[None, None, :]
    ).astype(jnp.bfloat16)
    return jnp.einsum(
        "ijt,tg->gij", one_hot, long_filter, preferred_element_type=jnp.float32
    ).astype(jnp.bfloat16)


def local(tokens, seq_lengths, in_weight, short_filter, long_filter, out_weight):
    rows, channels = tokens.shape
    width = short_filter.shape[0]
    filter_len, group_count = long_filter.shape
    per_group = channels // group_count
    n_seq = lax.axis_size("seq")
    s = lax.axis_index("seq")
    member = s % GROUP_DEVS
    part = LANE // GROUP_DEVS
    n_lblk = channels // LANE
    tail = filter_len + 8
    span = GROUP_DEVS * rows
    ext_rows = tail + span

    swaps = [[(i, i ^ d) for i in range(n_seq)] for d in range(1, GROUP_DEVS)]
    from_member = [tokens] + [lax.ppermute(tokens, "seq", perm) for perm in swaps]
    blocks = []
    for m in range(GROUP_DEVS):
        pick = from_member[0]
        for d in range(1, GROUP_DEVS):
            pick = jnp.where((member ^ d) == m, from_member[d], pick)
        blocks.append(pick)
    tail_src = tokens[rows - tail :]
    tail_tok = jnp.zeros_like(tail_src)
    for m in range(GROUP_DEVS):
        dist = m + 1
        perm = [(i - dist, i) for i in range(GROUP_DEVS, n_seq) if i % GROUP_DEVS == m]
        got = lax.ppermute(tail_src, "seq", perm)
        tail_tok = jnp.where(member == m, got, tail_tok)
    ext_tokens = jnp.concatenate([tail_tok] + blocks, axis=0)

    lengths_row = seq_lengths[0]
    seq_starts = jnp.cumsum(lengths_row) - lengths_row
    pair_start = (s // GROUP_DEVS) * span
    row_ids = pair_start - tail + jnp.arange(ext_rows, dtype=jnp.int32)
    position = positions(row_ids, seq_starts)

    offset = member * part
    w_t = in_weight.T.reshape(in_weight.shape[1] // LANE, LANE, channels)
    w_part = lax.dynamic_slice_in_dim(w_t, offset, part, axis=1)
    w_all = lax.all_gather(w_part, "fsdp", axis=0, tiled=True)
    own = n_lblk * part
    w_all = w_all.reshape(3 * own, channels)

    ow = out_weight.reshape(n_lblk, LANE, channels)
    weights = []
    for d in range(GROUP_DEVS):
        src_offset = (member ^ d) * part
        weights.append(lax.dynamic_slice_in_dim(ow, src_offset, part, axis=1).reshape(own, channels))
    ow_cat = jnp.concatenate(weights, axis=0)
    ext_tokens, ow_cat = lax.optimization_barrier((ext_tokens, ow_cat))
    projected = jnp.dot(
        ext_tokens, w_all.T, preferred_element_type=jnp.float32
    ).astype(jnp.bfloat16)

    taps = short_filter.reshape(width, 3, n_lblk, LANE)
    taps = lax.dynamic_slice_in_dim(taps, offset, part, axis=3).reshape(width, 3 * own)

    start = 8
    feat_rows = ext_rows - start
    pos_f = position[start:]
    featured = jnp.zeros((feat_rows, 3 * own), jnp.float32)
    for tap_index in range(width):
        shifted = projected[start - tap_index : ext_rows - tap_index].astype(jnp.float32)
        featured = featured + taps[tap_index] * jnp.where(
            (pos_f >= tap_index)[:, None], shifted, 0.0
        )
    queries = featured[feat_rows - span :, :own]
    mixed_in = (featured[:, own : 2 * own] * featured[:, 2 * own :]).astype(jnp.bfloat16)

    sub = LANE // per_group
    lf = long_filter.reshape(filter_len, n_lblk, sub)
    lf = lax.dynamic_slice_in_dim(lf, offset // per_group, part // per_group, axis=2)
    lf = lf.reshape(filter_len, own // per_group)
    n_groups = own // per_group

    out_rows = jnp.arange(filter_len, dtype=jnp.int32)[:, None]
    src_rows = jnp.arange(filter_len, dtype=jnp.int32)[None, :]
    cur_tap = out_rows - src_rows
    prev_tap = out_rows + filter_len - src_rows
    cur_table = tap_table(cur_tap, lf)
    prev_table = tap_table(prev_tap, lf)

    n_blocks = span // filter_len
    pos_out = position[tail:].reshape(n_blocks, filter_len)
    cur_kernel = jnp.where(
        (cur_tap[None] <= pos_out[:, :, None])[:, None], cur_table[None], 0.0
    ).astype(jnp.bfloat16)
    prev_kernel = jnp.where(
        (prev_tap[None] <= pos_out[:, :, None])[:, None], prev_table[None], 0.0
    ).astype(jnp.bfloat16)

    mi_t = mixed_in.T.reshape(n_groups, per_group, n_blocks + 1, filter_len)
    filtered = jnp.einsum(
        "gcbj,bgij->gcbi", mi_t[:, :, 1:], cur_kernel, preferred_element_type=jnp.float32
    )
    filtered = filtered + jnp.einsum(
        "gcbj,bgij->gcbi", mi_t[:, :, :-1], prev_kernel, preferred_element_type=jnp.float32
    )
    filtered = filtered.reshape(own, span)
    gated = (queries.T * filtered).astype(jnp.bfloat16)


    gated = gated.reshape(own, GROUP_DEVS, rows)
    result = tokens.astype(jnp.float32)
    for d in range(GROUP_DEVS):
        send = lax.dynamic_index_in_dim(gated, member ^ d, axis=1, keepdims=False)
        got = send if d == 0 else lax.ppermute(send, "seq", swaps[d - 1])
        result = result + lax.dot_general(
            got,
            ow_cat[d * own : (d + 1) * own],
            (((0,), (0,)), ((), ())),
            preferred_element_type=jnp.float32,
        )
    return result.astype(jnp.bfloat16)


def solution(mesh):
    in_specs = (P(("fsdp", "seq"), None), P("fsdp", None), P(None, "fsdp"), P(), P(), P())
    out_specs = P(("fsdp", "seq"), None)
    return jax.shard_map(local, mesh=mesh, in_specs=in_specs, out_specs=out_specs, check_vma=False)
```

```python
import jax
import jax.numpy as jnp
from jax import lax
from jax.sharding import PartitionSpec as P

LANE = 128
GROUP_DEVS = 4


def positions(row_ids, seq_starts):
    seq_begin = jnp.max(
        jnp.where(seq_starts[None, :] <= row_ids[:, None], seq_starts[None, :], 0), axis=1
    )
    return row_ids - seq_begin


def tap_table(tap_ids, long_filter):
    filter_len = long_filter.shape[0]
    one_hot = (
        tap_ids[:, :, None] == jnp.arange(filter_len, dtype=jnp.int32)[None, None, :]
    ).astype(jnp.bfloat16)
    return jnp.einsum(
        "ijt,tg->gij", one_hot, long_filter, preferred_element_type=jnp.float32
    ).astype(jnp.bfloat16)


def local(tokens, seq_lengths, in_weight, short_filter, long_filter, out_weight):
    rows, channels = tokens.shape
    width = short_filter.shape[0]
    filter_len, group_count = long_filter.shape
    per_group = channels // group_count
    n_seq = lax.axis_size("seq")
    s = lax.axis_index("seq")
    member = s % GROUP_DEVS
    part = LANE // GROUP_DEVS
    n_lblk = channels // LANE
    tail = filter_len + 8
    span = GROUP_DEVS * rows
    ext_rows = tail + span

    swaps = [[(i, i ^ d) for i in range(n_seq)] for d in range(1, GROUP_DEVS)]
    from_member = [tokens] + [lax.ppermute(tokens, "seq", perm) for perm in swaps]
    blocks = []
    for m in range(GROUP_DEVS):
        pick = from_member[0]
        for d in range(1, GROUP_DEVS):
            pick = jnp.where((member ^ d) == m, from_member[d], pick)
        blocks.append(pick)
    tail_src = tokens[rows - tail :]
    tail_tok = jnp.zeros_like(tail_src)
    for m in range(GROUP_DEVS):
        dist = m + 1
        perm = [(i - dist, i) for i in range(GROUP_DEVS, n_seq) if i % GROUP_DEVS == m]
        got = lax.ppermute(tail_src, "seq", perm)
        tail_tok = jnp.where(member == m, got, tail_tok)
    ext_tokens = jnp.concatenate([tail_tok] + blocks, axis=0)

    lengths_row = seq_lengths[0]
    seq_starts = jnp.cumsum(lengths_row) - lengths_row
    pair_start = (s // GROUP_DEVS) * span
    row_ids = pair_start - tail + jnp.arange(ext_rows, dtype=jnp.int32)
    position = positions(row_ids, seq_starts)

    offset = member * part
    w_t = in_weight.T.reshape(in_weight.shape[1] // LANE, LANE, channels)
    w_part = lax.dynamic_slice_in_dim(w_t, offset, part, axis=1)
    w_all = lax.all_gather(w_part, "fsdp", axis=0, tiled=True)
    own = n_lblk * part
    w_all = w_all.reshape(3 * own, channels)

    ow = out_weight.reshape(n_lblk, LANE, channels)
    weights = []
    for d in range(GROUP_DEVS):
        src_offset = (member ^ d) * part
        weights.append(lax.dynamic_slice_in_dim(ow, src_offset, part, axis=1).reshape(own, channels))
    ow_cat = jnp.concatenate(weights, axis=0)
    ext_tokens, ow_cat = lax.optimization_barrier((ext_tokens, ow_cat))
    projected = jnp.dot(
        ext_tokens, w_all.T, preferred_element_type=jnp.float32
    ).astype(jnp.bfloat16)

    taps = short_filter.reshape(width, 3, n_lblk, LANE)
    taps = lax.dynamic_slice_in_dim(taps, offset, part, axis=3).reshape(width, 3 * own)

    start = 8
    feat_rows = ext_rows - start
    pos_f = position[start:]
    featured = jnp.zeros((feat_rows, 3 * own), jnp.float32)
    for tap_index in range(width):
        shifted = projected[start - tap_index : ext_rows - tap_index].astype(jnp.float32)
        featured = featured + taps[tap_index] * jnp.where(
            (pos_f >= tap_index)[:, None], shifted, 0.0
        )
    queries = featured[feat_rows - span :, :own]
    mixed_in = (featured[:, own : 2 * own] * featured[:, 2 * own :]).astype(jnp.bfloat16)

    sub = LANE // per_group
    lf = long_filter.reshape(filter_len, n_lblk, sub)
    lf = lax.dynamic_slice_in_dim(lf, offset // per_group, part // per_group, axis=2)
    lf = lf.reshape(filter_len, own // per_group)
    n_groups = own // per_group

    out_rows = jnp.arange(filter_len, dtype=jnp.int32)[:, None]
    src_rows = jnp.arange(filter_len, dtype=jnp.int32)[None, :]
    cur_tap = out_rows - src_rows
    prev_tap = out_rows + filter_len - src_rows
    cur_table = tap_table(cur_tap, lf)
    prev_table = tap_table(prev_tap, lf)

    n_blocks = span // filter_len
    pos_out = position[tail:].reshape(n_blocks, filter_len)
    cur_kernel = jnp.where(
        (cur_tap[None] <= pos_out[:, :, None])[:, None], cur_table[None], 0.0
    ).astype(jnp.bfloat16)
    prev_kernel = jnp.where(
        (prev_tap[None] <= pos_out[:, :, None])[:, None], prev_table[None], 0.0
    ).astype(jnp.bfloat16)

    mi_t = mixed_in.T.reshape(n_groups, per_group, n_blocks + 1, filter_len)
    filtered = jnp.einsum(
        "gcbj,bgij->gbci", mi_t[:, :, 1:], cur_kernel, preferred_element_type=jnp.float32
    )
    filtered = filtered + jnp.einsum(
        "gcbj,bgij->gbci", mi_t[:, :, :-1], prev_kernel, preferred_element_type=jnp.float32
    )
    q_t = queries.reshape(n_blocks, filter_len, n_groups, per_group).transpose(2, 0, 3, 1)
    gated = (q_t * filtered).astype(jnp.bfloat16)

    per_member = rows // filter_len
    gated = gated.reshape(n_groups, GROUP_DEVS, per_member, per_group, filter_len)
    ow_cat = ow_cat.reshape(GROUP_DEVS, n_groups, per_group, channels)
    result = tokens.astype(jnp.float32)
    for d in range(GROUP_DEVS):
        send = lax.dynamic_index_in_dim(gated, member ^ d, axis=1, keepdims=False)
        got = send if d == 0 else lax.ppermute(send, "seq", swaps[d - 1])
        part_out = lax.dot_general(
            got, ow_cat[d], (((0, 2), (0, 1)), ((), ())), preferred_element_type=jnp.float32
        )
        result = result + part_out.reshape(rows, channels)
    return result.astype(jnp.bfloat16)


def solution(mesh):
    in_specs = (P(("fsdp", "seq"), None), P("fsdp", None), P(None, "fsdp"), P(), P(), P())
    out_specs = P(("fsdp", "seq"), None)
    return jax.shard_map(local, mesh=mesh, in_specs=in_specs, out_specs=out_specs, check_vma=False)
```

```python
import jax
import jax.numpy as jnp
from jax import lax
from jax.experimental import pallas as pl
from jax.experimental.pallas import tpu as pltpu
from jax.sharding import PartitionSpec as P
import functools

LANE = 128
GROUP_DEVS = 4


def positions(row_ids, seq_starts):
    seq_begin = jnp.max(
        jnp.where(seq_starts[None, :] <= row_ids[:, None], seq_starts[None, :], 0), axis=1
    )
    return row_ids - seq_begin


def tap_table(tap_ids, long_filter):
    filter_len = long_filter.shape[0]
    one_hot = (
        tap_ids[:, :, None] == jnp.arange(filter_len, dtype=jnp.int32)[None, None, :]
    ).astype(jnp.bfloat16)
    return jnp.einsum(
        "ijt,tg->gij", one_hot, long_filter, preferred_element_type=jnp.float32
    ).astype(jnp.bfloat16)


def proj_feat_kernel(tok_ref, w_ref, taps_ref, pos_ref, q_ref, mi_ref, proj_ref, *, width, start, n_out, chunk):
    for qkv in range(3):
        p = lax.dot_general(tok_ref[...], w_ref[qkv, 0], (((1,), (1,)), ((), ())),
                            preferred_element_type=jnp.float32)
        proj_ref[qkv] = p.astype(jnp.bfloat16).astype(jnp.float32)
    feat_rows = pos_ref.shape[0]
    q_first = feat_rows - n_out
    for c in range(feat_rows // chunk):
        lo = c * chunk
        pos = pos_ref[lo:lo + chunk, :]
        accs = []
        for qkv in range(3):
            if qkv == 0 and lo < q_first:
                accs.append(None)
                continue
            acc = None
            for t in range(width):
                sh = proj_ref[qkv, pl.ds(start + lo - t, chunk), :]
                term = taps_ref[t, qkv:qkv + 1, :] * jnp.where(pos >= t, sh, 0.0)
                acc = term if acc is None else acc + term
            accs.append(acc)
        if accs[0] is not None:
            q_ref[lo - q_first:lo - q_first + chunk, :] = accs[0]
        mi_ref[lo:lo + chunk, :] = (accs[1] * accs[2]).astype(mi_ref.dtype)


def proj_feat(ext_tokens, w4, taps3, pos_b, *, start, n_out, tile=128, chunk=128):
    ext_rows, d = ext_tokens.shape
    n_tiles = w4.shape[1]
    width = taps3.shape[0]
    feat_rows = pos_b.shape[0]
    kern = functools.partial(proj_feat_kernel, width=width, start=start, n_out=n_out, chunk=chunk)
    return pl.pallas_call(
        kern,
        grid=(n_tiles,),
        in_specs=[
            pl.BlockSpec((ext_rows, d), lambda j: (0, 0)),
            pl.BlockSpec((3, 1, tile, d), lambda j: (0, j, 0, 0)),
            pl.BlockSpec((width, 3, tile), lambda j: (0, 0, j)),
            pl.BlockSpec((feat_rows, tile), lambda j: (0, 0)),
        ],
        out_specs=[
            pl.BlockSpec((n_out, tile), lambda j: (0, j)),
            pl.BlockSpec((feat_rows, tile), lambda j: (0, j)),
        ],
        out_shape=[
            jax.ShapeDtypeStruct((n_out, n_tiles * tile), jnp.float32),
            jax.ShapeDtypeStruct((feat_rows, n_tiles * tile), jnp.bfloat16),
        ],
        scratch_shapes=[pltpu.VMEM((3, ext_rows, tile), jnp.float32)],
    )(ext_tokens, w4, taps3, pos_b)


def local(tokens, seq_lengths, in_weight, short_filter, long_filter, out_weight):
    rows, channels = tokens.shape
    width = short_filter.shape[0]
    filter_len, group_count = long_filter.shape
    per_group = channels // group_count
    n_seq = lax.axis_size("seq")
    s = lax.axis_index("seq")
    member = s % GROUP_DEVS
    part = LANE // GROUP_DEVS
    n_lblk = channels // LANE
    tail = filter_len + 8
    span = GROUP_DEVS * rows
    ext_rows = tail + span

    swaps = [[(i, i ^ d) for i in range(n_seq)] for d in range(1, GROUP_DEVS)]
    from_member = [tokens] + [lax.ppermute(tokens, "seq", perm) for perm in swaps]
    blocks = []
    for m in range(GROUP_DEVS):
        pick = from_member[0]
        for d in range(1, GROUP_DEVS):
            pick = jnp.where((member ^ d) == m, from_member[d], pick)
        blocks.append(pick)
    tail_src = tokens[rows - tail :]
    tail_tok = jnp.zeros_like(tail_src)
    for m in range(GROUP_DEVS):
        dist = m + 1
        perm = [(i - dist, i) for i in range(GROUP_DEVS, n_seq) if i % GROUP_DEVS == m]
        got = lax.ppermute(tail_src, "seq", perm)
        tail_tok = jnp.where(member == m, got, tail_tok)
    ext_tokens = jnp.concatenate([tail_tok] + blocks, axis=0)

    lengths_row = seq_lengths[0]
    seq_starts = jnp.cumsum(lengths_row) - lengths_row
    pair_start = (s // GROUP_DEVS) * span
    row_ids = pair_start - tail + jnp.arange(ext_rows, dtype=jnp.int32)
    position = positions(row_ids, seq_starts)

    offset = member * part
    w_t = in_weight.T.reshape(in_weight.shape[1] // LANE, LANE, channels)
    w_part = lax.dynamic_slice_in_dim(w_t, offset, part, axis=1)
    w_all = lax.all_gather(w_part, "fsdp", axis=0, tiled=True)
    own = n_lblk * part
    w_all = w_all.reshape(3 * own, channels)

    ow = out_weight.reshape(n_lblk, LANE, channels)
    weights = []
    for d in range(GROUP_DEVS):
        src_offset = (member ^ d) * part
        weights.append(lax.dynamic_slice_in_dim(ow, src_offset, part, axis=1).reshape(own, channels))
    ow_cat = jnp.concatenate(weights, axis=0)
    ext_tokens, ow_cat = lax.optimization_barrier((ext_tokens, ow_cat))
    taps = short_filter.reshape(width, 3, n_lblk, LANE)
    taps = lax.dynamic_slice_in_dim(taps, offset, part, axis=3).reshape(width, 3, own)
    start = 8
    feat_rows = ext_rows - start
    pos_b = jnp.broadcast_to(position[start:, None], (feat_rows, LANE))
    queries, mixed_in = proj_feat(
        ext_tokens, w_all.reshape(3, own // LANE, LANE, channels), taps, pos_b,
        start=start, n_out=span,
    )

    sub = LANE // per_group
    lf = long_filter.reshape(filter_len, n_lblk, sub)
    lf = lax.dynamic_slice_in_dim(lf, offset // per_group, part // per_group, axis=2)
    lf = lf.reshape(filter_len, own // per_group)
    n_groups = own // per_group

    out_rows = jnp.arange(filter_len, dtype=jnp.int32)[:, None]
    src_rows = jnp.arange(filter_len, dtype=jnp.int32)[None, :]
    cur_tap = out_rows - src_rows
    prev_tap = out_rows + filter_len - src_rows
    cur_table = tap_table(cur_tap, lf)
    prev_table = tap_table(prev_tap, lf)

    n_blocks = span // filter_len
    pos_out = position[tail:].reshape(n_blocks, filter_len)
    cur_kernel = jnp.where(
        (cur_tap[None] <= pos_out[:, :, None])[:, None], cur_table[None], 0.0
    ).astype(jnp.bfloat16)
    prev_kernel = jnp.where(
        (prev_tap[None] <= pos_out[:, :, None])[:, None], prev_table[None], 0.0
    ).astype(jnp.bfloat16)

    mi_t = mixed_in.T.reshape(n_groups, per_group, n_blocks + 1, filter_len)
    filtered = jnp.einsum(
        "gcbj,bgij->gcbi", mi_t[:, :, 1:], cur_kernel, preferred_element_type=jnp.float32
    )
    filtered = filtered + jnp.einsum(
        "gcbj,bgij->gcbi", mi_t[:, :, :-1], prev_kernel, preferred_element_type=jnp.float32
    )
    filtered = filtered.reshape(own, span)
    gated = (queries.T * filtered).astype(jnp.bfloat16)


    gated = gated.reshape(own, GROUP_DEVS, rows)
    pieces = []
    for d in range(GROUP_DEVS):
        send = lax.dynamic_index_in_dim(gated, member ^ d, axis=1, keepdims=False)
        got = send if d == 0 else lax.ppermute(send, "seq", swaps[d - 1])
        pieces.append(got)
    result = tokens.astype(jnp.float32) + lax.dot_general(
        jnp.concatenate(pieces, axis=0),
        ow_cat,
        (((0,), (0,)), ((), ())),
        preferred_element_type=jnp.float32,
    )
    return result.astype(jnp.bfloat16)


def solution(mesh):
    in_specs = (P(("fsdp", "seq"), None), P("fsdp", None), P(None, "fsdp"), P(), P(), P())
    out_specs = P(("fsdp", "seq"), None)
    return jax.shard_map(local, mesh=mesh, in_specs=in_specs, out_specs=out_specs, check_vma=False)
```

```python
import jax
import jax.numpy as jnp
from jax import lax
from jax.sharding import PartitionSpec as P

LANE = 128
GROUP_DEVS = 4


def positions(row_ids, seq_starts):
    seq_begin = jnp.max(
        jnp.where(seq_starts[None, :] <= row_ids[:, None], seq_starts[None, :], 0), axis=1
    )
    return row_ids - seq_begin


def tap_table(tap_ids, long_filter):
    filter_len = long_filter.shape[0]
    one_hot = (
        tap_ids[:, :, None] == jnp.arange(filter_len, dtype=jnp.int32)[None, None, :]
    ).astype(jnp.bfloat16)
    return jnp.einsum(
        "ijt,tg->gij", one_hot, long_filter, preferred_element_type=jnp.float32
    ).astype(jnp.bfloat16)


def local(tokens, seq_lengths, in_weight, short_filter, long_filter, out_weight):
    rows, channels = tokens.shape
    width = short_filter.shape[0]
    filter_len, group_count = long_filter.shape
    per_group = channels // group_count
    n_seq = lax.axis_size("seq")
    s = lax.axis_index("seq")
    member = s % GROUP_DEVS
    part = LANE // GROUP_DEVS
    n_lblk = channels // LANE
    tail = filter_len + 8
    span = GROUP_DEVS * rows
    ext_rows = tail + span

    swaps = [[(i, i ^ d) for i in range(n_seq)] for d in range(1, GROUP_DEVS)]
    from_member = [tokens] + [lax.ppermute(tokens, "seq", perm) for perm in swaps]
    blocks = []
    for m in range(GROUP_DEVS):
        pick = from_member[0]
        for d in range(1, GROUP_DEVS):
            pick = jnp.where((member ^ d) == m, from_member[d], pick)
        blocks.append(pick)
    tail_src = tokens[rows - tail :]
    tail_tok = jnp.zeros_like(tail_src)
    for m in range(GROUP_DEVS):
        dist = m + 1
        perm = [(i - dist, i) for i in range(GROUP_DEVS, n_seq) if i % GROUP_DEVS == m]
        got = lax.ppermute(tail_src, "seq", perm)
        tail_tok = jnp.where(member == m, got, tail_tok)
    ext_tokens = jnp.concatenate([tail_tok] + blocks, axis=0)

    lengths_row = seq_lengths[0]
    seq_starts = jnp.cumsum(lengths_row) - lengths_row
    pair_start = (s // GROUP_DEVS) * span
    row_ids = pair_start - tail + jnp.arange(ext_rows, dtype=jnp.int32)
    position = positions(row_ids, seq_starts)

    offset = member * part
    w_t = in_weight.T.reshape(in_weight.shape[1] // LANE, LANE, channels)
    w_part = lax.dynamic_slice_in_dim(w_t, offset, part, axis=1)
    w_all = lax.all_gather(w_part, "fsdp", axis=0, tiled=True)
    own = n_lblk * part
    w_all = w_all.reshape(3 * own, channels)

    ow = out_weight.reshape(n_lblk, LANE, channels)
    weights = []
    for d in range(GROUP_DEVS):
        src_offset = (member ^ d) * part
        weights.append(lax.dynamic_slice_in_dim(ow, src_offset, part, axis=1).reshape(own, channels))
    ow_cat = jnp.concatenate(weights, axis=0)
    ext_tokens, ow_cat = lax.optimization_barrier((ext_tokens, ow_cat))
    projected = jnp.dot(
        ext_tokens, w_all.T, preferred_element_type=jnp.float32
    ).astype(jnp.bfloat16)

    taps = short_filter.reshape(width, 3, n_lblk, LANE)
    taps = lax.dynamic_slice_in_dim(taps, offset, part, axis=3).reshape(width, 3 * own)

    start = 8
    feat_rows = ext_rows - start
    pos_f = position[start:]
    featured = jnp.zeros((feat_rows, 3 * own), jnp.float32)
    for tap_index in range(width):
        shifted = projected[start - tap_index : ext_rows - tap_index].astype(jnp.float32)
        featured = featured + taps[tap_index] * jnp.where(
            (pos_f >= tap_index)[:, None], shifted, 0.0
        )
    queries = featured[feat_rows - span :, :own]
    mixed_in = (featured[:, own : 2 * own] * featured[:, 2 * own :]).astype(jnp.bfloat16)

    sub = LANE // per_group
    lf = long_filter.reshape(filter_len, n_lblk, sub)
    lf = lax.dynamic_slice_in_dim(lf, offset // per_group, part // per_group, axis=2)
    lf = lf.reshape(filter_len, own // per_group)
    n_groups = own // per_group

    out_rows = jnp.arange(filter_len, dtype=jnp.int32)[:, None]
    src_rows = jnp.arange(filter_len, dtype=jnp.int32)[None, :]
    cur_tap = out_rows - src_rows
    prev_tap = out_rows + filter_len - src_rows
    cur_table = tap_table(cur_tap, lf)
    prev_table = tap_table(prev_tap, lf)

    n_blocks = span // filter_len
    pos_out = position[tail:].reshape(n_blocks, filter_len)
    window_kernel = jnp.where(
        jnp.concatenate(
            [
                jnp.broadcast_to(prev_tap[None] <= pos_out[:, :, None], (n_blocks,) + prev_tap.shape),
                jnp.broadcast_to(cur_tap[None] <= pos_out[:, :, None], (n_blocks,) + cur_tap.shape),
            ],
            axis=2,
        )[:, None],
        jnp.concatenate([prev_table, cur_table], axis=2)[None],
        0.0,
    ).astype(jnp.bfloat16)

    mi_t = mixed_in.T.reshape(n_groups, per_group, n_blocks + 1, filter_len)
    window = jnp.concatenate([mi_t[:, :, :-1], mi_t[:, :, 1:]], axis=3)
    filtered = jnp.einsum(
        "gcbj,bgij->gcbi", window, window_kernel, preferred_element_type=jnp.float32
    )
    filtered = filtered.reshape(own, span)
    gated = (queries.T * filtered).astype(jnp.bfloat16)


    gated = gated.reshape(own, GROUP_DEVS, rows)
    pieces = []
    for d in range(GROUP_DEVS):
        send = lax.dynamic_index_in_dim(gated, member ^ d, axis=1, keepdims=False)
        got = send if d == 0 else lax.ppermute(send, "seq", swaps[d - 1])
        pieces.append(got)
    result = tokens.astype(jnp.float32) + lax.dot_general(
        jnp.concatenate(pieces, axis=0),
        ow_cat,
        (((0,), (0,)), ((), ())),
        preferred_element_type=jnp.float32,
    )
    return result.astype(jnp.bfloat16)


def solution(mesh):
    in_specs = (P(("fsdp", "seq"), None), P("fsdp", None), P(None, "fsdp"), P(), P(), P())
    out_specs = P(("fsdp", "seq"), None)
    return jax.shard_map(local, mesh=mesh, in_specs=in_specs, out_specs=out_specs, check_vma=False)
```

```python
import jax
import jax.numpy as jnp
from jax import lax
from jax.sharding import PartitionSpec as P

LANE = 128
GROUP_DEVS = 4


def positions(row_ids, seq_starts):
    seq_begin = jnp.max(
        jnp.where(seq_starts[None, :] <= row_ids[:, None], seq_starts[None, :], 0), axis=1
    )
    return row_ids - seq_begin


def tap_table(tap_ids, long_filter):
    filter_len = long_filter.shape[0]
    one_hot = (
        tap_ids[:, :, None] == jnp.arange(filter_len, dtype=jnp.int32)[None, None, :]
    ).astype(jnp.bfloat16)
    return jnp.einsum(
        "ijt,tg->gij", one_hot, long_filter, preferred_element_type=jnp.float32
    ).astype(jnp.bfloat16)


def local(tokens, seq_lengths, in_weight, short_filter, long_filter, out_weight):
    rows, channels = tokens.shape
    width = short_filter.shape[0]
    filter_len, group_count = long_filter.shape
    per_group = channels // group_count
    n_seq = lax.axis_size("seq")
    s = lax.axis_index("seq")
    member = s % GROUP_DEVS
    part = LANE // GROUP_DEVS
    n_lblk = channels // LANE
    tail = filter_len + 8
    span = GROUP_DEVS * rows
    ext_rows = tail + span

    swaps = [[(i, i ^ d) for i in range(n_seq)] for d in range(1, GROUP_DEVS)]
    from_member = [tokens] + [lax.ppermute(tokens, "seq", perm) for perm in swaps]
    blocks = []
    for m in range(GROUP_DEVS):
        pick = from_member[0]
        for d in range(1, GROUP_DEVS):
            pick = jnp.where((member ^ d) == m, from_member[d], pick)
        blocks.append(pick)
    tail_src = tokens[rows - tail :]
    tail_tok = jnp.zeros_like(tail_src)
    for m in range(GROUP_DEVS):
        dist = m + 1
        perm = [(i - dist, i) for i in range(GROUP_DEVS, n_seq) if i % GROUP_DEVS == m]
        got = lax.ppermute(tail_src, "seq", perm)
        tail_tok = jnp.where(member == m, got, tail_tok)
    ext_tokens = jnp.concatenate([tail_tok] + blocks, axis=0)

    lengths_row = seq_lengths[0]
    seq_starts = jnp.cumsum(lengths_row) - lengths_row
    pair_start = (s // GROUP_DEVS) * span
    row_ids = pair_start - tail + jnp.arange(ext_rows, dtype=jnp.int32)
    position = positions(row_ids, seq_starts)

    offset = member * part
    w_t = in_weight.T.reshape(in_weight.shape[1] // LANE, LANE, channels)
    w_part = lax.dynamic_slice_in_dim(w_t, offset, part, axis=1)
    w_all = lax.all_gather(w_part, "fsdp", axis=0, tiled=True)
    own = n_lblk * part
    w_all = w_all.reshape(3 * own, channels)

    ow = out_weight.reshape(n_lblk, LANE, channels)
    weights = []
    for d in range(GROUP_DEVS):
        src_offset = (member ^ d) * part
        weights.append(lax.dynamic_slice_in_dim(ow, src_offset, part, axis=1).reshape(own, channels))
    ow_cat = jnp.concatenate(weights, axis=0)
    ext_tokens, ow_cat = lax.optimization_barrier((ext_tokens, ow_cat))
    projected = jnp.dot(
        ext_tokens, w_all.T, preferred_element_type=jnp.float32
    ).astype(jnp.bfloat16)

    taps = short_filter.reshape(width, 3, n_lblk, LANE)
    taps = lax.dynamic_slice_in_dim(taps, offset, part, axis=3).reshape(width, 3 * own)

    start = 8
    feat_rows = ext_rows - start
    pos_f = position[start:]
    featured = jnp.zeros((feat_rows, 3 * own), jnp.float32)
    for tap_index in range(width):
        shifted = projected[start - tap_index : ext_rows - tap_index].astype(jnp.float32)
        featured = featured + taps[tap_index] * jnp.where(
            (pos_f >= tap_index)[:, None], shifted, 0.0
        )
    queries = featured[feat_rows - span :, :own]
    mixed_in = (featured[:, own : 2 * own] * featured[:, 2 * own :]).astype(jnp.bfloat16)

    sub = LANE // per_group
    lf = long_filter.reshape(filter_len, n_lblk, sub)
    lf = lax.dynamic_slice_in_dim(lf, offset // per_group, part // per_group, axis=2)
    lf = lf.reshape(filter_len, own // per_group)
    n_groups = own // per_group

    out_rows = jnp.arange(filter_len, dtype=jnp.int32)[:, None]
    src_rows = jnp.arange(filter_len, dtype=jnp.int32)[None, :]
    cur_tap = out_rows - src_rows
    prev_tap = out_rows + filter_len - src_rows
    cur_table = tap_table(cur_tap, lf)
    prev_table = tap_table(prev_tap, lf)

    n_blocks = span // filter_len
    pos_out = position[tail:].reshape(n_blocks, filter_len)
    cur_kernel = jnp.where(
        (cur_tap[None] <= pos_out[:, :, None])[:, None], cur_table[None], 0.0
    ).astype(jnp.bfloat16)
    prev_kernel = jnp.where(
        (prev_tap[None] <= pos_out[:, :, None])[:, None], prev_table[None], 0.0
    ).astype(jnp.bfloat16)

    mi_t = mixed_in.T.reshape(n_groups, per_group, n_blocks + 1, filter_len)
    q_t = queries.T
    half_blocks = n_blocks // 2
    half_rows = span // 2

    def conv_half(h, mi_t, cur_kernel, prev_kernel, q_t):
        src = lax.dynamic_slice_in_dim(mi_t, h * half_blocks, half_blocks + 1, axis=2)
        ck = lax.dynamic_slice_in_dim(cur_kernel, h * half_blocks, half_blocks, axis=0)
        pk = lax.dynamic_slice_in_dim(prev_kernel, h * half_blocks, half_blocks, axis=0)
        filtered = jnp.einsum(
            "gcbj,bgij->gcbi", src[:, :, 1:], ck, preferred_element_type=jnp.float32
        )
        filtered = filtered + jnp.einsum(
            "gcbj,bgij->gcbi", src[:, :, :-1], pk, preferred_element_type=jnp.float32
        )
        q = lax.dynamic_slice_in_dim(q_t, h * half_rows, half_rows, axis=1)
        gated = (q * filtered.reshape(own, half_rows)).astype(jnp.bfloat16)
        return gated.reshape(own, 2, rows)

    chip = member // 2
    far = conv_half(1 - chip, mi_t, cur_kernel, prev_kernel, q_t)
    got = {}
    for d in (2, 3):
        send = lax.dynamic_index_in_dim(far, (member ^ d) % 2, axis=1, keepdims=False)
        got[d] = lax.ppermute(send, "seq", swaps[d - 1])
    far, mi_t, cur_kernel, prev_kernel, q_t = lax.optimization_barrier(
        (far, mi_t, cur_kernel, prev_kernel, q_t)
    )
    near = conv_half(chip, mi_t, cur_kernel, prev_kernel, q_t)
    got[0] = lax.dynamic_index_in_dim(near, member % 2, axis=1, keepdims=False)
    send = lax.dynamic_index_in_dim(near, (member ^ 1) % 2, axis=1, keepdims=False)
    got[1] = lax.ppermute(send, "seq", swaps[0])
    result = tokens.astype(jnp.float32)
    for d in range(GROUP_DEVS):
        result = result + lax.dot_general(
            got[d],
            ow_cat[d * own : (d + 1) * own],
            (((0,), (0,)), ((), ())),
            preferred_element_type=jnp.float32,
        )
    return result.astype(jnp.bfloat16)


def solution(mesh):
    in_specs = (P(("fsdp", "seq"), None), P("fsdp", None), P(None, "fsdp"), P(), P(), P())
    out_specs = P(("fsdp", "seq"), None)
    return jax.shard_map(local, mesh=mesh, in_specs=in_specs, out_specs=out_specs, check_vma=False)
```

```python
import jax
import jax.numpy as jnp
from jax import lax
from jax.sharding import PartitionSpec as P

LANE = 128
GROUP_DEVS = 4


def positions(row_ids, seq_starts):
    seq_begin = jnp.max(
        jnp.where(seq_starts[None, :] <= row_ids[:, None], seq_starts[None, :], 0), axis=1
    )
    return row_ids - seq_begin


def tap_table(tap_ids, long_filter):
    filter_len = long_filter.shape[0]
    one_hot = (
        tap_ids[:, :, None] == jnp.arange(filter_len, dtype=jnp.int32)[None, None, :]
    ).astype(jnp.bfloat16)
    return jnp.einsum(
        "ijt,tg->gij", one_hot, long_filter, preferred_element_type=jnp.float32
    ).astype(jnp.bfloat16)


def local(tokens, seq_lengths, in_weight, short_filter, long_filter, out_weight):
    rows, channels = tokens.shape
    width = short_filter.shape[0]
    filter_len, group_count = long_filter.shape
    per_group = channels // group_count
    n_seq = lax.axis_size("seq")
    s = lax.axis_index("seq")
    member = s % GROUP_DEVS
    part = LANE // GROUP_DEVS
    n_lblk = channels // LANE
    tail = filter_len + 8
    span = GROUP_DEVS * rows
    ext_rows = tail + span

    swaps = [[(i, i ^ d) for i in range(n_seq)] for d in range(1, GROUP_DEVS)]
    from_member = [tokens] + [lax.ppermute(tokens, "seq", perm) for perm in swaps]
    blocks = []
    for m in range(GROUP_DEVS):
        pick = from_member[0]
        for d in range(1, GROUP_DEVS):
            pick = jnp.where((member ^ d) == m, from_member[d], pick)
        blocks.append(pick)
    tail_src = tokens[rows - tail :]
    tail_tok = jnp.zeros_like(tail_src)
    for m in range(GROUP_DEVS):
        dist = m + 1
        perm = [(i - dist, i) for i in range(GROUP_DEVS, n_seq) if i % GROUP_DEVS == m]
        got = lax.ppermute(tail_src, "seq", perm)
        tail_tok = jnp.where(member == m, got, tail_tok)
    ext_tokens = jnp.concatenate([tail_tok] + blocks, axis=0)

    lengths_row = seq_lengths[0]
    seq_starts = jnp.cumsum(lengths_row) - lengths_row
    pair_start = (s // GROUP_DEVS) * span
    row_ids = pair_start - tail + jnp.arange(ext_rows, dtype=jnp.int32)
    position = positions(row_ids, seq_starts)

    offset = member * part
    w_t = in_weight.T.reshape(in_weight.shape[1] // LANE, LANE, channels)
    w_part = lax.dynamic_slice_in_dim(w_t, offset, part, axis=1)
    w_all = lax.all_gather(w_part, "fsdp", axis=0, tiled=True)
    own = n_lblk * part
    w_all = w_all.reshape(3 * own, channels)

    ow = out_weight.reshape(n_lblk, LANE, channels)
    weights = []
    for d in range(GROUP_DEVS):
        src_offset = (member ^ d) * part
        weights.append(lax.dynamic_slice_in_dim(ow, src_offset, part, axis=1).reshape(own, channels))
    ow_cat = jnp.concatenate(weights, axis=0)
    ext_tokens, ow_cat = lax.optimization_barrier((ext_tokens, ow_cat))
    projected = jnp.dot(
        ext_tokens, w_all.T, preferred_element_type=jnp.float32
    ).astype(jnp.bfloat16)

    taps = short_filter.reshape(width, 3, n_lblk, LANE)
    taps = lax.dynamic_slice_in_dim(taps, offset, part, axis=3).reshape(width, 3 * own)

    start = 8
    feat_rows = ext_rows - start
    pos_f = position[start:]
    featured = jnp.zeros((feat_rows, 3 * own), jnp.float32)
    for tap_index in range(width):
        shifted = projected[start - tap_index : ext_rows - tap_index].astype(jnp.float32)
        featured = featured + taps[tap_index] * jnp.where(
            (pos_f >= tap_index)[:, None], shifted, 0.0
        )
    queries = featured[feat_rows - span :, :own]
    mixed_in = (featured[:, own : 2 * own] * featured[:, 2 * own :]).astype(jnp.bfloat16)

    sub = LANE // per_group
    lf = long_filter.reshape(filter_len, n_lblk, sub)
    lf = lax.dynamic_slice_in_dim(lf, offset // per_group, part // per_group, axis=2)
    lf = lf.reshape(filter_len, own // per_group)
    n_groups = own // per_group

    out_rows = jnp.arange(filter_len, dtype=jnp.int32)[:, None]
    src_rows = jnp.arange(filter_len, dtype=jnp.int32)[None, :]
    cur_tap = out_rows - src_rows
    prev_tap = out_rows + filter_len - src_rows
    cur_table = tap_table(cur_tap, lf)
    prev_table = tap_table(prev_tap, lf)

    n_blocks = span // filter_len
    mi_blocks = mixed_in.reshape(n_blocks + 1, filter_len, n_groups, per_group)
    pos_out = position[tail:].reshape(n_blocks, filter_len)
    cur_kernel = jnp.where(
        (cur_tap[None] <= pos_out[:, :, None])[:, None], cur_table[None], 0.0
    ).astype(jnp.bfloat16)
    prev_kernel = jnp.where(
        (prev_tap[None] <= pos_out[:, :, None])[:, None], prev_table[None], 0.0
    ).astype(jnp.bfloat16)
    filtered = jnp.einsum(
        "bgij,bjgc->bigc", cur_kernel, mi_blocks[1:], preferred_element_type=jnp.float32
    )
    filtered = filtered + jnp.einsum(
        "bgij,bjgc->bigc", prev_kernel, mi_blocks[:-1], preferred_element_type=jnp.float32
    )
    filtered = filtered.reshape(span, own)
    gated = (queries * filtered).astype(jnp.bfloat16)

    gated = gated.reshape(GROUP_DEVS, rows, own)
    pieces = []
    for d in range(GROUP_DEVS):
        send = lax.dynamic_index_in_dim(gated, member ^ d, axis=0, keepdims=False)
        got = send if d == 0 else lax.ppermute(send, "seq", swaps[d - 1])
        pieces.append(got)
    result = tokens.astype(jnp.float32) + jnp.dot(
        jnp.concatenate(pieces, axis=1), ow_cat, preferred_element_type=jnp.float32
    )
    return result.astype(jnp.bfloat16)


def solution(mesh):
    in_specs = (P(("fsdp", "seq"), None), P("fsdp", None), P(None, "fsdp"), P(), P(), P())
    out_specs = P(("fsdp", "seq"), None)
    return jax.shard_map(local, mesh=mesh, in_specs=in_specs, out_specs=out_specs, check_vma=False)
```

```python
import jax
import jax.numpy as jnp
from jax import lax
from jax.sharding import PartitionSpec as P

LANE = 128
GROUP_DEVS = 4


def positions(row_ids, seq_starts):
    seq_begin = jnp.max(
        jnp.where(seq_starts[None, :] <= row_ids[:, None], seq_starts[None, :], 0), axis=1
    )
    return row_ids - seq_begin


def tap_table(tap_ids, long_filter):
    filter_len = long_filter.shape[0]
    one_hot = (
        tap_ids[:, :, None] == jnp.arange(filter_len, dtype=jnp.int32)[None, None, :]
    ).astype(jnp.bfloat16)
    return jnp.einsum(
        "ijt,tg->gij", one_hot, long_filter, preferred_element_type=jnp.float32
    ).astype(jnp.bfloat16)


def local(tokens, seq_lengths, in_weight, short_filter, long_filter, out_weight):
    rows, channels = tokens.shape
    width = short_filter.shape[0]
    filter_len, group_count = long_filter.shape
    per_group = channels // group_count
    n_seq = lax.axis_size("seq")
    s = lax.axis_index("seq")
    member = s % GROUP_DEVS
    part = LANE // GROUP_DEVS
    n_lblk = channels // LANE
    tail = filter_len + 8
    span = GROUP_DEVS * rows
    ext_rows = tail + span

    swaps = [[(i, i ^ d) for i in range(n_seq)] for d in range(1, GROUP_DEVS)]
    from_member = [tokens] + [lax.ppermute(tokens, "seq", perm) for perm in swaps]
    blocks = []
    for m in range(GROUP_DEVS):
        pick = from_member[0]
        for d in range(1, GROUP_DEVS):
            pick = jnp.where((member ^ d) == m, from_member[d], pick)
        blocks.append(pick)
    tail_src = tokens[rows - tail :]
    tail_tok = jnp.zeros_like(tail_src)
    for m in range(GROUP_DEVS):
        dist = m + 1
        perm = [(i - dist, i) for i in range(GROUP_DEVS, n_seq) if i % GROUP_DEVS == m]
        got = lax.ppermute(tail_src, "seq", perm)
        tail_tok = jnp.where(member == m, got, tail_tok)
    ext_tokens = jnp.concatenate([tail_tok] + blocks, axis=0)

    lengths_row = seq_lengths[0]
    seq_starts = jnp.cumsum(lengths_row) - lengths_row
    pair_start = (s // GROUP_DEVS) * span
    row_ids = pair_start - tail + jnp.arange(ext_rows, dtype=jnp.int32)
    position = positions(row_ids, seq_starts)

    offset = member * part
    w_t = in_weight.T.reshape(in_weight.shape[1] // LANE, LANE, channels)
    w_part = lax.dynamic_slice_in_dim(w_t, offset, part, axis=1)
    w_all = lax.all_gather(w_part, "fsdp", axis=0, tiled=True)
    own = n_lblk * part
    w_all = w_all.reshape(3 * own, channels)

    ow = out_weight.reshape(n_lblk, LANE, channels)
    weights = []
    for d in range(GROUP_DEVS):
        src_offset = (member ^ d) * part
        weights.append(lax.dynamic_slice_in_dim(ow, src_offset, part, axis=1).reshape(own, channels))
    ow_cat = jnp.concatenate(weights, axis=0)
    ext_tokens, ow_cat = lax.optimization_barrier((ext_tokens, ow_cat))
    projected = jnp.dot(
        ext_tokens, w_all.T, preferred_element_type=jnp.float32
    ).astype(jnp.bfloat16)

    taps = short_filter.reshape(width, 3, n_lblk, LANE)
    taps = lax.dynamic_slice_in_dim(taps, offset, part, axis=3).reshape(width, 3 * own)

    start = 8
    feat_rows = ext_rows - start
    pos_f = position[start:]
    featured = jnp.zeros((feat_rows, 3 * own), jnp.float32)
    for tap_index in range(width):
        shifted = projected[start - tap_index : ext_rows - tap_index].astype(jnp.float32)
        featured = featured + taps[tap_index] * jnp.where(
            (pos_f >= tap_index)[:, None], shifted, 0.0
        )
    queries = featured[feat_rows - span :, :own]
    mixed_in = (featured[:, own : 2 * own] * featured[:, 2 * own :]).astype(jnp.bfloat16)

    sub = LANE // per_group
    lf = long_filter.reshape(filter_len, n_lblk, sub)
    lf = lax.dynamic_slice_in_dim(lf, offset // per_group, part // per_group, axis=2)
    lf = lf.reshape(filter_len, own // per_group)
    n_groups = own // per_group

    out_rows = jnp.arange(filter_len, dtype=jnp.int32)[:, None]
    src_rows = jnp.arange(filter_len, dtype=jnp.int32)[None, :]
    cur_tap = out_rows - src_rows
    prev_tap = out_rows + filter_len - src_rows
    cur_table = tap_table(cur_tap, lf)
    prev_table = tap_table(prev_tap, lf)

    n_blocks = span // filter_len
    pos_out = position[tail:].reshape(n_blocks, filter_len)
    cur_kernel = jnp.where(
        (cur_tap[None] <= pos_out[:, :, None])[:, None], cur_table[None], 0.0
    ).astype(jnp.bfloat16)
    prev_kernel = jnp.where(
        (prev_tap[None] <= pos_out[:, :, None])[:, None], prev_table[None], 0.0
    ).astype(jnp.bfloat16)

    mi_t = mixed_in.T.reshape(n_groups, per_group, n_blocks + 1, filter_len)
    filtered = jnp.einsum(
        "gcbj,bgij->gcbi", mi_t[:, :, 1:], cur_kernel, preferred_element_type=jnp.float32
    )
    filtered = filtered + jnp.einsum(
        "gcbj,bgij->gcbi", mi_t[:, :, :-1], prev_kernel, preferred_element_type=jnp.float32
    )
    filtered = filtered.reshape(own, span)
    gated = (queries.T * filtered).astype(jnp.bfloat16)


    gated = gated.T.reshape(GROUP_DEVS, rows, own)
    pieces = []
    for d in range(GROUP_DEVS):
        send = lax.dynamic_index_in_dim(gated, member ^ d, axis=0, keepdims=False)
        got = send if d == 0 else lax.ppermute(send, "seq", swaps[d - 1])
        pieces.append(got)
    result = tokens.astype(jnp.float32) + jnp.dot(
        jnp.concatenate(pieces, axis=1), ow_cat, preferred_element_type=jnp.float32
    )
    return result.astype(jnp.bfloat16)


def solution(mesh):
    in_specs = (P(("fsdp", "seq"), None), P("fsdp", None), P(None, "fsdp"), P(), P(), P())
    out_specs = P(("fsdp", "seq"), None)
    return jax.shard_map(local, mesh=mesh, in_specs=in_specs, out_specs=out_specs, check_vma=False)
```

```python
import jax
import jax.numpy as jnp
from jax import lax
from jax.sharding import PartitionSpec as P

LANE = 128
GROUP_DEVS = 4


def positions(row_ids, seq_starts):
    seq_begin = jnp.max(
        jnp.where(seq_starts[None, :] <= row_ids[:, None], seq_starts[None, :], 0), axis=1
    )
    return row_ids - seq_begin


def tap_table(tap_ids, long_filter):
    filter_len = long_filter.shape[0]
    one_hot = (
        tap_ids[:, :, None] == jnp.arange(filter_len, dtype=jnp.int32)[None, None, :]
    ).astype(jnp.bfloat16)
    return jnp.einsum(
        "ijt,tg->gij", one_hot, long_filter, preferred_element_type=jnp.float32
    ).astype(jnp.bfloat16)


def local(tokens, seq_lengths, in_weight, short_filter, long_filter, out_weight):
    rows, channels = tokens.shape
    width = short_filter.shape[0]
    filter_len, group_count = long_filter.shape
    per_group = channels // group_count
    n_seq = lax.axis_size("seq")
    s = lax.axis_index("seq")
    member = s % GROUP_DEVS
    part = LANE // GROUP_DEVS
    n_lblk = channels // LANE
    tail = filter_len + 8
    span = GROUP_DEVS * rows
    ext_rows = tail + span

    swaps = [[(i, i ^ d) for i in range(n_seq)] for d in range(1, GROUP_DEVS)]
    from_member = [tokens] + [lax.ppermute(tokens, "seq", perm) for perm in swaps]
    blocks = []
    for m in range(GROUP_DEVS):
        pick = from_member[0]
        for d in range(1, GROUP_DEVS):
            pick = jnp.where((member ^ d) == m, from_member[d], pick)
        blocks.append(pick)
    tail_src = tokens[rows - tail :]
    tail_tok = jnp.zeros_like(tail_src)
    for m in range(GROUP_DEVS):
        dist = m + 1
        perm = [(i - dist, i) for i in range(GROUP_DEVS, n_seq) if i % GROUP_DEVS == m]
        got = lax.ppermute(tail_src, "seq", perm)
        tail_tok = jnp.where(member == m, got, tail_tok)
    ext_tokens = jnp.concatenate([tail_tok] + blocks, axis=0)

    lengths_row = seq_lengths[0]
    seq_starts = jnp.cumsum(lengths_row) - lengths_row
    pair_start = (s // GROUP_DEVS) * span
    row_ids = pair_start - tail + jnp.arange(ext_rows, dtype=jnp.int32)
    position = positions(row_ids, seq_starts)

    offset = member * part
    w_t = in_weight.T.reshape(in_weight.shape[1] // LANE, LANE, channels)
    w_part = lax.dynamic_slice_in_dim(w_t, offset, part, axis=1)
    w_all = lax.all_gather(w_part, "fsdp", axis=0, tiled=True)
    own = n_lblk * part
    w_all = w_all.reshape(3 * own, channels)

    ow = out_weight.reshape(n_lblk, LANE, channels)
    weights = []
    for d in range(GROUP_DEVS):
        src_offset = (member ^ d) * part
        weights.append(lax.dynamic_slice_in_dim(ow, src_offset, part, axis=1).reshape(own, channels))
    ow_cat = jnp.concatenate(weights, axis=0)
    ext_tokens, ow_cat = lax.optimization_barrier((ext_tokens, ow_cat))
    projected = jnp.dot(
        ext_tokens, w_all.T, preferred_element_type=jnp.float32
    ).astype(jnp.bfloat16)

    taps = short_filter.reshape(width, 3, n_lblk, LANE)
    taps = lax.dynamic_slice_in_dim(taps, offset, part, axis=3).reshape(width, 3 * own)

    start = 8
    feat_rows = ext_rows - start
    pos_f = position[start:]
    featured = jnp.zeros((feat_rows, 3 * own), jnp.float32)
    for tap_index in range(width):
        shifted = projected[start - tap_index : ext_rows - tap_index].astype(jnp.float32)
        featured = featured + taps[tap_index] * jnp.where(
            (pos_f >= tap_index)[:, None], shifted, 0.0
        )
    queries = featured[feat_rows - span :, :own]
    mixed_in = (featured[:, own : 2 * own] * featured[:, 2 * own :]).astype(jnp.bfloat16)

    sub = LANE // per_group
    lf = long_filter.reshape(filter_len, n_lblk, sub)
    lf = lax.dynamic_slice_in_dim(lf, offset // per_group, part // per_group, axis=2)
    lf = lf.reshape(filter_len, own // per_group)
    n_groups = own // per_group

    out_rows = jnp.arange(filter_len, dtype=jnp.int32)[:, None]
    src_rows = jnp.arange(filter_len, dtype=jnp.int32)[None, :]
    cur_tap = out_rows - src_rows
    prev_tap = out_rows + filter_len - src_rows
    cur_table = tap_table(cur_tap, lf)
    prev_table = tap_table(prev_tap, lf)

    n_blocks = span // filter_len
    pos_out = position[tail:].reshape(n_blocks, filter_len)
    cur_kernel = jnp.where(
        (cur_tap[None] <= pos_out[:, :, None])[:, None], cur_table[None], 0.0
    ).astype(jnp.bfloat16)
    prev_kernel = jnp.where(
        (prev_tap[None] <= pos_out[:, :, None])[:, None], prev_table[None], 0.0
    ).astype(jnp.bfloat16)

    mi_t = mixed_in.T.reshape(n_groups, per_group, n_blocks + 1, filter_len)
    filtered = jnp.einsum(
        "gcbj,bgij->gcbi", mi_t[:, :, 1:], cur_kernel, preferred_element_type=jnp.float32
    )
    filtered = filtered + jnp.einsum(
        "gcbj,bgij->gcbi", mi_t[:, :, :-1], prev_kernel, preferred_element_type=jnp.float32
    )
    filtered = filtered.reshape(own, span)
    gated = (queries.T * filtered).astype(jnp.bfloat16)


    gated = gated.T.reshape(GROUP_DEVS, rows, own)
    result = tokens.astype(jnp.float32)
    for d in range(GROUP_DEVS):
        send = lax.dynamic_index_in_dim(gated, member ^ d, axis=0, keepdims=False)
        got = send if d == 0 else lax.ppermute(send, "seq", swaps[d - 1])
        result = result + jnp.dot(
            got, ow_cat[d * own : (d + 1) * own], preferred_element_type=jnp.float32
        )
    return result.astype(jnp.bfloat16)


def solution(mesh):
    in_specs = (P(("fsdp", "seq"), None), P("fsdp", None), P(None, "fsdp"), P(), P(), P())
    out_specs = P(("fsdp", "seq"), None)
    return jax.shard_map(local, mesh=mesh, in_specs=in_specs, out_specs=out_specs, check_vma=False)
```

```python
import jax
import jax.numpy as jnp
from jax import lax
from jax.sharding import PartitionSpec as P

LANE = 128
GROUP_DEVS = 4


def positions(row_ids, seq_starts):
    seq_begin = jnp.max(
        jnp.where(seq_starts[None, :] <= row_ids[:, None], seq_starts[None, :], 0), axis=1
    )
    return row_ids - seq_begin


def tap_table(tap_ids, long_filter):
    filter_len = long_filter.shape[0]
    one_hot = (
        tap_ids[:, :, None] == jnp.arange(filter_len, dtype=jnp.int32)[None, None, :]
    ).astype(jnp.bfloat16)
    return jnp.einsum(
        "ijt,tg->gij", one_hot, long_filter, preferred_element_type=jnp.float32
    ).astype(jnp.bfloat16)


def local(tokens, seq_lengths, in_weight, short_filter, long_filter, out_weight):
    rows, channels = tokens.shape
    width = short_filter.shape[0]
    filter_len, group_count = long_filter.shape
    per_group = channels // group_count
    n_seq = lax.axis_size("seq")
    s = lax.axis_index("seq")
    member = s % GROUP_DEVS
    part = LANE // GROUP_DEVS
    n_lblk = channels // LANE
    tail = filter_len + 8
    span = GROUP_DEVS * rows
    ext_rows = tail + span

    swaps = [[(i, i ^ d) for i in range(n_seq)] for d in range(1, GROUP_DEVS)]
    from_member = [tokens, lax.ppermute(tokens, "seq", swaps[0])]
    for d in range(2, GROUP_DEVS, 2):
        fetched = lax.ppermute(tokens, "seq", swaps[d - 1])
        from_member += [fetched, lax.ppermute(fetched, "seq", swaps[0])]
    blocks = []
    for m in range(GROUP_DEVS):
        pick = from_member[0]
        for d in range(1, GROUP_DEVS):
            pick = jnp.where((member ^ d) == m, from_member[d], pick)
        blocks.append(pick)
    tail_src = tokens[rows - tail :]
    tail_tok = jnp.zeros_like(tail_src)
    for m in range(GROUP_DEVS):
        dist = m + 1
        perm = [(i - dist, i) for i in range(GROUP_DEVS, n_seq) if i % GROUP_DEVS == m]
        got = lax.ppermute(tail_src, "seq", perm)
        tail_tok = jnp.where(member == m, got, tail_tok)
    ext_tokens = jnp.concatenate([tail_tok] + blocks, axis=0)

    lengths_row = seq_lengths[0]
    seq_starts = jnp.cumsum(lengths_row) - lengths_row
    pair_start = (s // GROUP_DEVS) * span
    row_ids = pair_start - tail + jnp.arange(ext_rows, dtype=jnp.int32)
    position = positions(row_ids, seq_starts)

    offset = member * part
    w_t = in_weight.T.reshape(in_weight.shape[1] // LANE, LANE, channels)
    w_part = lax.dynamic_slice_in_dim(w_t, offset, part, axis=1)
    w_all = lax.all_gather(w_part, "fsdp", axis=0, tiled=True)
    own = n_lblk * part
    w_all = w_all.reshape(3 * own, channels)

    ow = out_weight.reshape(n_lblk, LANE, channels)
    weights = []
    for d in range(GROUP_DEVS):
        src_offset = (member ^ d) * part
        weights.append(lax.dynamic_slice_in_dim(ow, src_offset, part, axis=1).reshape(own, channels))
    ow_cat = jnp.concatenate(weights, axis=0)
    ext_tokens, ow_cat = lax.optimization_barrier((ext_tokens, ow_cat))
    projected = jnp.dot(
        ext_tokens, w_all.T, preferred_element_type=jnp.float32
    ).astype(jnp.bfloat16)

    taps = short_filter.reshape(width, 3, n_lblk, LANE)
    taps = lax.dynamic_slice_in_dim(taps, offset, part, axis=3).reshape(width, 3 * own)

    start = 8
    feat_rows = ext_rows - start
    pos_f = position[start:]
    featured = jnp.zeros((feat_rows, 3 * own), jnp.float32)
    for tap_index in range(width):
        shifted = projected[start - tap_index : ext_rows - tap_index].astype(jnp.float32)
        featured = featured + taps[tap_index] * jnp.where(
            (pos_f >= tap_index)[:, None], shifted, 0.0
        )
    queries = featured[feat_rows - span :, :own]
    mixed_in = (featured[:, own : 2 * own] * featured[:, 2 * own :]).astype(jnp.bfloat16)

    sub = LANE // per_group
    lf = long_filter.reshape(filter_len, n_lblk, sub)
    lf = lax.dynamic_slice_in_dim(lf, offset // per_group, part // per_group, axis=2)
    lf = lf.reshape(filter_len, own // per_group)
    n_groups = own // per_group

    out_rows = jnp.arange(filter_len, dtype=jnp.int32)[:, None]
    src_rows = jnp.arange(filter_len, dtype=jnp.int32)[None, :]
    cur_tap = out_rows - src_rows
    prev_tap = out_rows + filter_len - src_rows
    cur_table = tap_table(cur_tap, lf)
    prev_table = tap_table(prev_tap, lf)

    n_blocks = span // filter_len
    pos_out = position[tail:].reshape(n_blocks, filter_len)
    cur_kernel = jnp.where(
        (cur_tap[None] <= pos_out[:, :, None])[:, None], cur_table[None], 0.0
    ).astype(jnp.bfloat16)
    prev_kernel = jnp.where(
        (prev_tap[None] <= pos_out[:, :, None])[:, None], prev_table[None], 0.0
    ).astype(jnp.bfloat16)

    mi_t = mixed_in.T.reshape(n_groups, per_group, n_blocks + 1, filter_len)
    filtered = jnp.einsum(
        "gcbj,bgij->gcbi", mi_t[:, :, 1:], cur_kernel, preferred_element_type=jnp.float32
    )
    filtered = filtered + jnp.einsum(
        "gcbj,bgij->gcbi", mi_t[:, :, :-1], prev_kernel, preferred_element_type=jnp.float32
    )
    filtered = filtered.reshape(own, span)
    gated = (queries.T * filtered).astype(jnp.bfloat16)


    gated = gated.T.reshape(GROUP_DEVS, rows, own)
    pieces = []
    for d in range(GROUP_DEVS):
        send = lax.dynamic_index_in_dim(gated, member ^ d, axis=0, keepdims=False)
        got = send if d == 0 else lax.ppermute(send, "seq", swaps[d - 1])
        pieces.append(got)
    result = tokens.astype(jnp.float32) + jnp.dot(
        jnp.concatenate(pieces, axis=1), ow_cat, preferred_element_type=jnp.float32
    )
    return result.astype(jnp.bfloat16)


def solution(mesh):
    in_specs = (P(("fsdp", "seq"), None), P("fsdp", None), P(None, "fsdp"), P(), P(), P())
    out_specs = P(("fsdp", "seq"), None)
    return jax.shard_map(local, mesh=mesh, in_specs=in_specs, out_specs=out_specs, check_vma=False)
```

```python
import jax
import jax.numpy as jnp
from jax import lax
from jax.sharding import PartitionSpec as P

LANE = 128
GROUP_DEVS = 4


def positions(row_ids, seq_starts):
    seq_begin = jnp.max(
        jnp.where(seq_starts[None, :] <= row_ids[:, None], seq_starts[None, :], 0), axis=1
    )
    return row_ids - seq_begin


def tap_table(tap_ids, long_filter):
    filter_len = long_filter.shape[0]
    one_hot = (
        tap_ids[:, :, None] == jnp.arange(filter_len, dtype=jnp.int32)[None, None, :]
    ).astype(jnp.bfloat16)
    return jnp.einsum(
        "ijt,tg->gij", one_hot, long_filter, preferred_element_type=jnp.float32
    ).astype(jnp.bfloat16)


def local(tokens, seq_lengths, in_weight, short_filter, long_filter, out_weight):
    rows, channels = tokens.shape
    width = short_filter.shape[0]
    filter_len, group_count = long_filter.shape
    per_group = channels // group_count
    n_seq = lax.axis_size("seq")
    s = lax.axis_index("seq")
    member = s % GROUP_DEVS
    part = LANE // GROUP_DEVS
    n_lblk = channels // LANE
    tail = filter_len + 8
    span = GROUP_DEVS * rows
    ext_rows = tail + span

    swaps = [[(i, i ^ d) for i in range(n_seq)] for d in range(1, GROUP_DEVS)]
    from_member = [tokens, lax.ppermute(tokens, "seq", swaps[0])]
    for d in range(2, GROUP_DEVS, 2):
        fetched = lax.ppermute(tokens, "seq", swaps[d - 1])
        from_member += [fetched, lax.ppermute(fetched, "seq", swaps[0])]
    blocks = []
    for m in range(GROUP_DEVS):
        pick = from_member[0]
        for d in range(1, GROUP_DEVS):
            pick = jnp.where((member ^ d) == m, from_member[d], pick)
        blocks.append(pick)
    tail_src = tokens[rows - tail :]
    tail_tok = jnp.zeros_like(tail_src)
    for m in range(GROUP_DEVS):
        dist = m + 1
        perm = [(i - dist, i) for i in range(GROUP_DEVS, n_seq) if i % GROUP_DEVS == m]
        got = lax.ppermute(tail_src, "seq", perm)
        tail_tok = jnp.where(member == m, got, tail_tok)
    ext_tokens = jnp.concatenate([tail_tok] + blocks, axis=0)

    lengths_row = seq_lengths[0]
    seq_starts = jnp.cumsum(lengths_row) - lengths_row
    pair_start = (s // GROUP_DEVS) * span
    row_ids = pair_start - tail + jnp.arange(ext_rows, dtype=jnp.int32)
    position = positions(row_ids, seq_starts)

    offset = member * part
    w_t = in_weight.T.reshape(in_weight.shape[1] // LANE, LANE, channels)
    w_part = lax.dynamic_slice_in_dim(w_t, offset, part, axis=1)
    w_all = lax.all_gather(w_part, "fsdp", axis=0, tiled=True)
    own = n_lblk * part
    w_all = w_all.reshape(3 * own, channels)

    ow = out_weight.reshape(n_lblk, LANE, channels)
    weights = []
    for d in range(GROUP_DEVS):
        src_offset = (member ^ d) * part
        weights.append(lax.dynamic_slice_in_dim(ow, src_offset, part, axis=1).reshape(own, channels))
    ow_cat = jnp.concatenate(weights, axis=0)
    ext_tokens, ow_cat = lax.optimization_barrier((ext_tokens, ow_cat))
    projected = jnp.dot(
        ext_tokens, w_all.T, preferred_element_type=jnp.float32
    ).astype(jnp.bfloat16)

    taps = short_filter.reshape(width, 3, n_lblk, LANE)
    taps = lax.dynamic_slice_in_dim(taps, offset, part, axis=3).reshape(width, 3 * own)

    start = 8
    feat_rows = ext_rows - start
    pos_f = position[start:]
    featured = jnp.zeros((feat_rows, 3 * own), jnp.float32)
    for tap_index in range(width):
        shifted = projected[start - tap_index : ext_rows - tap_index].astype(jnp.float32)
        featured = featured + taps[tap_index] * jnp.where(
            (pos_f >= tap_index)[:, None], shifted, 0.0
        )
    queries = featured[feat_rows - span :, :own]
    mixed_in = (featured[:, own : 2 * own] * featured[:, 2 * own :]).astype(jnp.bfloat16)

    sub = LANE // per_group
    lf = long_filter.reshape(filter_len, n_lblk, sub)
    lf = lax.dynamic_slice_in_dim(lf, offset // per_group, part // per_group, axis=2)
    lf = lf.reshape(filter_len, own // per_group)
    n_groups = own // per_group

    out_rows = jnp.arange(filter_len, dtype=jnp.int32)[:, None]
    src_rows = jnp.arange(filter_len, dtype=jnp.int32)[None, :]
    cur_tap = out_rows - src_rows
    prev_tap = out_rows + filter_len - src_rows
    cur_table = tap_table(cur_tap, lf)
    prev_table = tap_table(prev_tap, lf)

    n_blocks = span // filter_len
    pos_out = position[tail:].reshape(n_blocks, filter_len)
    cur_kernel = jnp.where(
        (cur_tap[None] <= pos_out[:, :, None])[:, None], cur_table[None], 0.0
    ).astype(jnp.bfloat16)
    prev_kernel = jnp.where(
        (prev_tap[None] <= pos_out[:, :, None])[:, None], prev_table[None], 0.0
    ).astype(jnp.bfloat16)

    mi_t = mixed_in.T.reshape(n_groups, per_group, n_blocks + 1, filter_len)
    filtered = jnp.einsum(
        "gcbj,bgij->gcbi", mi_t[:, :, 1:], cur_kernel, preferred_element_type=jnp.float32
    )
    filtered = filtered + jnp.einsum(
        "gcbj,bgij->gcbi", mi_t[:, :, :-1], prev_kernel, preferred_element_type=jnp.float32
    )
    filtered = filtered.reshape(own, span)
    gated = (queries.T * filtered).astype(jnp.bfloat16)


    gated = gated.T.reshape(GROUP_DEVS, rows, own)
    result = tokens.astype(jnp.float32)
    for d in range(GROUP_DEVS):
        send = lax.dynamic_index_in_dim(gated, member ^ d, axis=0, keepdims=False)
        got = send if d == 0 else lax.ppermute(send, "seq", swaps[d - 1])
        result = result + jnp.dot(
            got, ow_cat[d * own : (d + 1) * own], preferred_element_type=jnp.float32
        )
    return result.astype(jnp.bfloat16)


def solution(mesh):
    in_specs = (P(("fsdp", "seq"), None), P("fsdp", None), P(None, "fsdp"), P(), P(), P())
    out_specs = P(("fsdp", "seq"), None)
    return jax.shard_map(local, mesh=mesh, in_specs=in_specs, out_specs=out_specs, check_vma=False)
```

```python
import jax
import jax.numpy as jnp
from jax import lax
from jax.sharding import PartitionSpec as P

LANE = 128
GROUP_DEVS = 4


def positions(row_ids, seq_starts):
    seq_begin = jnp.max(
        jnp.where(seq_starts[None, :] <= row_ids[:, None], seq_starts[None, :], 0), axis=1
    )
    return row_ids - seq_begin


def tap_table(tap_ids, long_filter):
    filter_len = long_filter.shape[0]
    one_hot = (
        tap_ids[:, :, None] == jnp.arange(filter_len, dtype=jnp.int32)[None, None, :]
    ).astype(jnp.bfloat16)
    return jnp.einsum(
        "ijt,tg->gij", one_hot, long_filter, preferred_element_type=jnp.float32
    ).astype(jnp.bfloat16)


def local(tokens, seq_lengths, in_weight, short_filter, long_filter, out_weight):
    rows, channels = tokens.shape
    width = short_filter.shape[0]
    filter_len, group_count = long_filter.shape
    per_group = channels // group_count
    n_seq = lax.axis_size("seq")
    s = lax.axis_index("seq")
    member = s % GROUP_DEVS
    part = LANE // GROUP_DEVS
    n_lblk = channels // LANE
    tail = filter_len + 8
    span = GROUP_DEVS * rows
    ext_rows = tail + span

    swaps = [[(i, i ^ d) for i in range(n_seq)] for d in range(1, GROUP_DEVS)]
    from_member = [tokens, lax.ppermute(tokens, "seq", swaps[0])]
    for d in range(2, GROUP_DEVS, 2):
        fetched = lax.ppermute(tokens, "seq", swaps[d - 1])
        from_member += [fetched, lax.ppermute(fetched, "seq", swaps[0])]
    blocks = []
    for m in range(GROUP_DEVS):
        pick = from_member[0]
        for d in range(1, GROUP_DEVS):
            pick = jnp.where((member ^ d) == m, from_member[d], pick)
        blocks.append(pick)
    tail_src = tokens[rows - tail :]
    tail_tok = jnp.zeros_like(tail_src)
    for m in range(GROUP_DEVS):
        dist = m + 1
        perm = [(i - dist, i) for i in range(GROUP_DEVS, n_seq) if i % GROUP_DEVS == m]
        got = lax.ppermute(tail_src, "seq", perm)
        tail_tok = jnp.where(member == m, got, tail_tok)
    ext_tokens = jnp.concatenate([tail_tok] + blocks, axis=0)

    lengths_row = seq_lengths[0]
    seq_starts = jnp.cumsum(lengths_row) - lengths_row
    pair_start = (s // GROUP_DEVS) * span
    row_ids = pair_start - tail + jnp.arange(ext_rows, dtype=jnp.int32)
    position = positions(row_ids, seq_starts)

    offset = member * part
    w_t = in_weight.T.reshape(in_weight.shape[1] // LANE, LANE, channels)
    w_part = lax.dynamic_slice_in_dim(w_t, offset, part, axis=1)
    w_all = lax.all_gather(w_part, "fsdp", axis=0, tiled=True)
    own = n_lblk * part
    w_all = w_all.reshape(3 * own, channels)

    ow = out_weight.reshape(n_lblk, LANE, channels)
    weights = []
    for d in range(GROUP_DEVS):
        src_offset = (member ^ d) * part
        weights.append(lax.dynamic_slice_in_dim(ow, src_offset, part, axis=1).reshape(own, channels))
    ow_cat = jnp.concatenate(weights, axis=0)
    ext_tokens, ow_cat = lax.optimization_barrier((ext_tokens, ow_cat))
    projected = jnp.dot(
        ext_tokens, w_all.T, preferred_element_type=jnp.float32
    ).astype(jnp.bfloat16)

    taps = short_filter.reshape(width, 3, n_lblk, LANE)
    taps = lax.dynamic_slice_in_dim(taps, offset, part, axis=3).reshape(width, 3 * own)

    start = 8
    feat_rows = ext_rows - start
    pos_f = position[start:]
    featured = jnp.zeros((feat_rows, 3 * own), jnp.float32)
    for tap_index in range(width):
        shifted = projected[start - tap_index : ext_rows - tap_index].astype(jnp.float32)
        featured = featured + taps[tap_index] * shifted
    fix_rows = 8
    for k in range(seq_starts.shape[0]):
        first = jnp.clip(seq_starts[k] - (pair_start - tail) - start, 0, feat_rows - fix_rows)
        src = lax.dynamic_slice_in_dim(
            projected, first + start - (width - 1), fix_rows + width - 1, axis=0
        ).astype(jnp.float32)
        pos_w = lax.dynamic_slice_in_dim(pos_f, first, fix_rows, axis=0)
        fix = jnp.zeros((fix_rows, 3 * own), jnp.float32)
        for tap_index in range(width):
            piece = src[width - 1 - tap_index : width - 1 - tap_index + fix_rows]
            fix = fix + taps[tap_index] * jnp.where((pos_w >= tap_index)[:, None], piece, 0.0)
        featured = lax.dynamic_update_slice_in_dim(featured, fix, first, axis=0)
    queries = featured[feat_rows - span :, :own]
    mixed_in = (featured[:, own : 2 * own] * featured[:, 2 * own :]).astype(jnp.bfloat16)

    sub = LANE // per_group
    lf = long_filter.reshape(filter_len, n_lblk, sub)
    lf = lax.dynamic_slice_in_dim(lf, offset // per_group, part // per_group, axis=2)
    lf = lf.reshape(filter_len, own // per_group)
    n_groups = own // per_group

    out_rows = jnp.arange(filter_len, dtype=jnp.int32)[:, None]
    src_rows = jnp.arange(filter_len, dtype=jnp.int32)[None, :]
    cur_tap = out_rows - src_rows
    prev_tap = out_rows + filter_len - src_rows
    cur_table = tap_table(cur_tap, lf)
    prev_table = tap_table(prev_tap, lf)

    n_blocks = span // filter_len
    pos_out = position[tail:].reshape(n_blocks, filter_len)
    cur_kernel = jnp.where(
        (cur_tap[None] <= pos_out[:, :, None])[:, None], cur_table[None], 0.0
    ).astype(jnp.bfloat16)
    prev_kernel = jnp.where(
        (prev_tap[None] <= pos_out[:, :, None])[:, None], prev_table[None], 0.0
    ).astype(jnp.bfloat16)

    mi_t = mixed_in.T.reshape(n_groups, per_group, n_blocks + 1, filter_len)
    filtered = jnp.einsum(
        "gcbj,bgij->gcbi", mi_t[:, :, 1:], cur_kernel, preferred_element_type=jnp.float32
    )
    filtered = filtered + jnp.einsum(
        "gcbj,bgij->gcbi", mi_t[:, :, :-1], prev_kernel, preferred_element_type=jnp.float32
    )
    filtered = filtered.reshape(own, span)
    gated = (queries.T * filtered).astype(jnp.bfloat16)


    gated = gated.T.reshape(GROUP_DEVS, rows, own)
    pieces = []
    for d in range(GROUP_DEVS):
        send = lax.dynamic_index_in_dim(gated, member ^ d, axis=0, keepdims=False)
        got = send if d == 0 else lax.ppermute(send, "seq", swaps[d - 1])
        pieces.append(got)
    result = tokens.astype(jnp.float32) + jnp.dot(
        jnp.concatenate(pieces, axis=1), ow_cat, preferred_element_type=jnp.float32
    )
    return result.astype(jnp.bfloat16)


def solution(mesh):
    in_specs = (P(("fsdp", "seq"), None), P("fsdp", None), P(None, "fsdp"), P(), P(), P())
    out_specs = P(("fsdp", "seq"), None)
    return jax.shard_map(local, mesh=mesh, in_specs=in_specs, out_specs=out_specs, check_vma=False)
```
